512 devices in a mesh: pipe: 16 (over z, core), expert: 32 (over x, y).
Axes of the slice: x: 4, y: 8, z: 8, core: 2. Of those that a mesh axis runs over, the one named last changes fastest.
Arguments:
- acts: bfloat16 [16, 2048, 3584], P('pipe', 'expert'), may hold values from -6 to 6
- norm_gain: bfloat16 [16, 3584], P('pipe'), may hold values from 0.5 to 1.5
- gate_w: bfloat16 [16, 32, 3584, 128], P('pipe', 'expert'), may hold values from -0.09375 to 0.09375
- up_w: bfloat16 [16, 32, 3584, 128], P('pipe', 'expert'), may hold values from -0.09375 to 0.09375
- down_w: bfloat16 [16, 32, 128, 3584], P('pipe', 'expert'), may hold values from -0.1875 to 0.1875
- route_ids: int32 [16, 2, 2048, 1], P('pipe', None, 'expert'), may hold values from 0 to 3; in each aligned block of 64 rows (0 to 63, 64 to 127, ..., all dimensions but the last counted through in order) at most 17 rows name the same one
- route_wts: int32 [16, 2, 2048, 1], P('pipe', None, 'expert'), may hold values from 512 to 2047
Outputs:
- out: bfloat16 [16, 2048, 3584], P('pipe', 'expert')
The draws below stay inside these ranges and needn't reach their ends.
Inputs may be any that keep to these rules, and one draw needn't show every extreme that they name: `route_ids`: within one row the 1 expert differ. In each aligned block of 64 rows (one device's rows of one section and tick), no expert is named by more than 17 rows; in some blocks an expert is named by exactly 17.
All inputs are finite; a program needn't handle non-finite values.
Results may differ from the reference program's by a relative error of at most 0.0052.
Values may be sent and summed in bfloat16 or wider, within the bound.
No kernel may reach another device: no remote copies, remote signals or barrier semaphores. Data moves between devices by JAX's collectives and lax.ppermute only.
A program may use at most 64 MiB of HBM per device.

```python
import math
import jax
import jax.numpy as jnp
import numpy as np
from jax import lax

D = 3584
HID = 1024
TOPK = 1
EXPERTS = 4
ROWS = 64
SECTIONS = 16
GROUP = 8
HSLICE = 128
TOK = 2048
MOST = 17
N_EXPERT = 32


def plant(result, own_key, smallest, high):
    spot = [jax.random.randint(jax.random.fold_in(own_key, axis), (), 0, length) for axis, length in enumerate(result.shape)]
    main_axis = result.shape.index(max(result.shape))
    beside = spot[:main_axis] + [(spot[main_axis] + 1) % result.shape[main_axis]] + spot[main_axis + 1:]
    return result.at[tuple(spot)].set(smallest).at[tuple(beside)].set(high)


def level_of(rng, extent, cuts, least, largest):
    loudness, own = 1.0, jax.random.fold_in(rng, 6)
    for axis_at, parts in cuts:
        draws = jnp.exp(jax.random.uniform(jax.random.fold_in(own, axis_at), (parts,), jnp.float32, least / len(cuts), largest / len(cuts)))
        loudness = loudness * jnp.repeat(draws, extent[axis_at] // parts).reshape([-1 if axis == axis_at else 1 for axis in range(len(extent))])
    return loudness


def assign_block(key, own, number, rows, number_of, top, reach, lean):
    order = jax.random.permutation(key, number_of)
    packed, common = portions_of(number_of, rows * top, reach, lean, True), portions_of(number_of, rows * top, reach, lean, False)
    places = jnp.arange(number_of)

    def named(tallies, rotation):
        used = int((tallies > 0).sum())
        fixed = max(1, used // 4)
        moved = fixed + (places - fixed + rotation * (used - fixed)) % max(1, number_of - fixed)
        return jnp.zeros((number_of,), jnp.int32).at[order[jnp.where(places < fixed, places, moved)]].set(jnp.asarray(tallies, jnp.int32))

    tallies = jnp.where(number % 4 == 0, named(packed, number // 4), named(common, number - number // 4 - 1))
    mixed = jax.random.permutation(jax.random.fold_in(own, 3), number_of)
    donor, receiver = mixed[0:number_of // 2 * 2:2], mixed[1:number_of // 2 * 2:2]
    slack = jnp.minimum(tallies[donor] - 1, reach - tallies[receiver]) // 2
    slack = jnp.where((donor == order[0]) | (receiver == order[0]) | (tallies[receiver] == 0), 0, jnp.maximum(slack, 0))
    moved = jax.random.randint(jax.random.fold_in(own, 4), (number_of // 2,), 0, 1 << 20) % (slack + 1)
    tallies = tallies.at[donor].add(-moved).at[receiver].add(moved)
    items = jnp.searchsorted(jnp.cumsum(tallies), jnp.arange(rows * top), side="right").astype(jnp.int32)
    listing = items.reshape(top, rows).T
    listing = listing[jax.random.permutation(jax.random.fold_in(own, 1), rows)]
    rotation = jax.random.randint(jax.random.fold_in(own, 2), (rows, 1), 0, top)
    return jnp.take_along_axis(listing, (jnp.arange(top)[None, :] + rotation) % top, axis=1)


def portions_of(amount, total, bound, lean, full):
    portions = [(1 << 20) // math.isqrt(grade ** lean) + 1 for grade in range(1, amount + 1)]
    largest = bound if full else min(bound, max(-(-total // amount), total * portions[0] // sum(portions)))
    least = 1 if total - largest >= amount - 1 else 0
    holding, rest = [largest] + [least] * (amount - 1), total - largest - least * (amount - 1)
    while rest > 0:
        movable = [i for i in range(1, amount) if holding[i] < largest] or [i for i in range(1, amount) if holding[i] < bound]
        mass, remaining = sum([portions[i] for i in movable]), rest
        for i in movable:
            addition = min(bound - holding[i], max(1, remaining * portions[i] // mass), rest)
            holding[i] = holding[i] + addition
            rest = rest - addition
    return np.array(holding)


def gaussian(rng, shape, deviation, most, cuts=(), kind=jnp.bfloat16):
    result = jax.random.normal(rng, shape, jnp.float32) * deviation
    if len(cuts) > 0:
        result = level_of(rng, shape, cuts, -0.22, 0.18) * result
    return jnp.clip(result, min=-most, max=most).astype(kind)


def setup_inputs(seed: int = 0) -> dict:
    streams_of = jax.random.split(jax.random.key(seed), 8)
    acts = gaussian(streams_of[0], (SECTIONS, TOK, D), 1.0, 6.0, ((0, 16), (1, 32)))
    norm_gain = jnp.clip(1.0 + 0.1 * jax.random.normal(streams_of[1], (SECTIONS, D), jnp.float32), 0.5, 1.5).astype(jnp.bfloat16)
    gate_w = gaussian(streams_of[2], (SECTIONS, EXPERTS * GROUP, D, HSLICE), D ** -0.5, 0.09375, ((0, 16), (1, 32)))
    up_w = gaussian(streams_of[3], (SECTIONS, EXPERTS * GROUP, D, HSLICE), D ** -0.5, 0.09375, ((0, 16), (1, 32)))
    down_w = gaussian(streams_of[4], (SECTIONS, EXPERTS * GROUP, HSLICE, D), HID ** -0.5, 0.1875, ((0, 16), (1, 32)))
    route_ids_keys = jax.random.split(jax.random.fold_in(streams_of[5], 1), SECTIONS * 2 * TOK // ROWS)
    route_ids_turns = jax.random.permutation(jax.random.fold_in(streams_of[5], 3), SECTIONS * 2 * TOK // ROWS)
    route_ids = jax.vmap(lambda own, number: assign_block(jax.random.fold_in(streams_of[5], 2), own, number, ROWS, EXPERTS, TOPK, MOST, 2))(route_ids_keys, route_ids_turns).reshape((SECTIONS, 2, TOK, TOPK))
    route_wts = plant(jax.random.randint(streams_of[6], (SECTIONS, 2, TOK, TOPK), 512, 2048), jax.random.fold_in(streams_of[6], 1), 512, 2047).astype(jnp.int32)
    return dict(acts=acts, norm_gain=norm_gain, gate_w=gate_w, up_w=up_w, down_w=down_w, route_ids=route_ids, route_wts=route_wts)


NORM_EPS = 1e-06
FIXED_UNIT = 1.0 / 4096.0

def slot_index(expert_ids, capacity, experts):
    flat_ids = expert_ids.reshape(-1)
    onehot = (flat_ids[:, None] == jnp.arange(experts, dtype=jnp.int32)[None, :]).astype(jnp.int32)
    before = jnp.cumsum(onehot, axis=0) - onehot
    slot_rank = lax.optimization_barrier(jnp.sum(before * onehot, axis=1))
    return (flat_ids * capacity + slot_rank).reshape(expert_ids.shape).astype(jnp.int32)

def place_rows(normed, slot_ids, slot_total):
    slot_marks = slot_ids[:, :, None] == jnp.arange(slot_total, dtype=jnp.int32)[None, None, :]
    placing = lax.optimization_barrier(jnp.sum(slot_marks.astype(jnp.float32), axis=1)).T.astype(jnp.bfloat16)
    return jnp.dot(placing, normed, preferred_element_type=jnp.float32).astype(jnp.bfloat16)

def serve_expert(operands):
    slot_rows, gate_slices, up_slices, down_slices = operands

    def add_slice(summed, slice_weights):
        w_gate, w_up, w_down = slice_weights
        gate_act = jnp.dot(slot_rows, w_gate, preferred_element_type=jnp.float32)
        up_act = jnp.dot(slot_rows, w_up, preferred_element_type=jnp.float32)
        hidden = (jax.nn.silu(gate_act) * up_act).astype(jnp.bfloat16)
        slice_part = jnp.dot(hidden, w_down, preferred_element_type=jnp.float32).astype(jnp.bfloat16)
        return (summed + slice_part.astype(jnp.float32), None)
    start_sum = jnp.zeros((slot_rows.shape[0], D), jnp.float32)
    summed, unused_out = lax.scan(add_slice, start_sum, (gate_slices, up_slices, down_slices))
    return summed

def section_layer(operands):
    rows_in, gain_row, w_gate, w_up, w_down, expert_ids, route_weight = operands
    values = rows_in.astype(jnp.float32)
    inv_rms = lax.rsqrt(lax.optimization_barrier(jnp.mean(values * values, axis=1, keepdims=True)) + NORM_EPS)
    normed = (values * inv_rms * gain_row.astype(jnp.float32)).astype(jnp.bfloat16)
    sources = normed.reshape(N_EXPERT, ROWS, D)
    id_blocks = expert_ids.reshape(N_EXPERT, ROWS, TOPK)
    slot_ids = jax.vmap(lambda block_ids: slot_index(block_ids, MOST, EXPERTS))(id_blocks)
    buffers = jax.vmap(lambda source_rows, source_slots: place_rows(source_rows, source_slots, EXPERTS * MOST))(sources, slot_ids)
    per_expert = buffers.reshape(N_EXPERT, EXPERTS, MOST, D).transpose(1, 0, 2, 3).reshape(EXPERTS, N_EXPERT * MOST, D)
    gate_groups = w_gate.reshape(EXPERTS, GROUP, D, HSLICE)
    up_groups = w_up.reshape(EXPERTS, GROUP, D, HSLICE)
    down_groups = w_down.reshape(EXPERTS, GROUP, HSLICE, D)
    served = lax.map(serve_expert, (per_expert, gate_groups, up_groups, down_groups))
    returned = served.reshape(EXPERTS, N_EXPERT, MOST, D).transpose(1, 0, 2, 3).reshape(N_EXPERT, EXPERTS * MOST, D)
    picked = jax.vmap(lambda back_rows, source_slots: back_rows[source_slots])(returned, slot_ids)
    weights = route_weight.reshape(N_EXPERT, ROWS, TOPK).astype(jnp.float32) * FIXED_UNIT
    branch = lax.optimization_barrier(jnp.sum(weights[..., None] * picked, axis=2)).reshape(TOK, D)
    return (values + branch).astype(jnp.bfloat16)

def reference(acts, norm_gain, gate_w, up_w, down_w, route_ids, route_wts):
    first_out = lax.map(section_layer, (acts, norm_gain, gate_w, up_w, down_w, route_ids[:, 0], route_wts[:, 0]))
    arrived = jnp.roll(first_out, 1, axis=0)
    second = lax.map(section_layer, (arrived[1:], norm_gain[1:], gate_w[1:], up_w[1:], down_w[1:], route_ids[1:, 1], route_wts[1:, 1]))
    return jnp.concatenate([arrived[:1], second], axis=0)
```

```python
import jax
import jax.numpy as jnp
from jax import lax
from jax.sharding import Mesh
from jax.sharding import PartitionSpec as P

EXPERTS = 4
MOST = 17


NORM_EPS = 1e-06
FIXED_UNIT = 1.0 / 4096.0


def shifted(value, axis, steps):
    count = lax.axis_size(axis)
    pairs = [(source, (source + steps) % count) for source in range(count)]
    return lax.ppermute(value, axis, pairs)


def slot_index(expert_ids, capacity, experts):
    flat_ids = expert_ids.reshape(-1)
    onehot = (flat_ids[:, None] == jnp.arange(experts, dtype=jnp.int32)[None, :]).astype(jnp.int32)
    before = jnp.cumsum(onehot, axis=0) - onehot
    slot_rank = jnp.sum(before * onehot, axis=1)
    return (flat_ids * capacity + slot_rank).reshape(expert_ids.shape)


def place_rows(normed, slot_ids, slot_total):
    slot_marks = slot_ids[:, :, None] == jnp.arange(slot_total, dtype=jnp.int32)[None, None, :]
    placing = jnp.sum(slot_marks.astype(jnp.float32), axis=1).T.astype(jnp.bfloat16)
    return jnp.dot(placing, normed, preferred_element_type=jnp.float32).astype(jnp.bfloat16)


def routed_branch(normed, expert_ids, route_weight, w_gate, w_up, down_all):
    n_x = lax.axis_size("ex")
    model_width = normed.shape[1]
    slot_ids = slot_index(expert_ids, MOST, EXPERTS)
    per_expert = place_rows(normed, slot_ids, EXPERTS * MOST).reshape(EXPERTS, MOST, model_width)
    from_x = lax.all_to_all(per_expert, "ex", split_axis=0, concat_axis=0, tiled=True)
    slot_rows = lax.all_gather(from_x, "ey", axis=0, tiled=False)
    n_y = slot_rows.shape[0]
    flat_rows = slot_rows.reshape(-1, model_width)
    gate_act = jnp.dot(flat_rows, w_gate, preferred_element_type=jnp.float32)
    up_act = jnp.dot(flat_rows, w_up, preferred_element_type=jnp.float32)
    hidden = (jax.nn.silu(gate_act) * up_act).astype(jnp.bfloat16)
    hidden = hidden.reshape(n_y, n_x * MOST, hidden.shape[-1])
    hidden_here = lax.all_to_all(hidden, "ey", split_axis=0, concat_axis=0, tiled=True)
    parts = jnp.einsum("jrh,jhd->jrd", hidden_here, down_all, preferred_element_type=jnp.float32)
    expert_out = jnp.sum(parts.astype(jnp.bfloat16).astype(jnp.float32), axis=0)
    expert_out = expert_out.reshape(n_x, MOST, model_width)
    returned = lax.all_to_all(expert_out, "ex", split_axis=0, concat_axis=0, tiled=True)
    picked = returned.reshape(EXPERTS * MOST, model_width)[slot_ids]
    weights = route_weight.astype(jnp.float32) * FIXED_UNIT
    return jnp.sum(weights[:, :, None] * picked, axis=1)


def layer_terms(rows_in, gain_row, w_gate, w_up, down_all, expert_ids, route_weight):
    values = rows_in.astype(jnp.float32)
    inv_rms = lax.rsqrt(jnp.mean(values * values, axis=1, keepdims=True) + NORM_EPS)
    normed = (values * inv_rms * gain_row.astype(jnp.float32)).astype(jnp.bfloat16)
    branch = routed_branch(normed, expert_ids, route_weight, w_gate, w_up, down_all)
    return (values, branch)


def shards(acts, norm_gain, gate_w, up_w, down_w, route_ids, route_wts):
    section_index = lax.axis_index("pipe")
    rows_in = acts[0]
    gain_row = norm_gain[0]
    w_gate = gate_w[0, 0]
    w_up = up_w[0, 0]
    down_all = lax.all_gather(down_w[0, 0], "ey", axis=0, tiled=False)
    values, branch = layer_terms(
        rows_in, gain_row, w_gate, w_up, down_all, route_ids[0, 0], route_wts[0, 0]
    )
    first_out = (values + branch).astype(jnp.bfloat16)
    arrived = shifted(first_out, "pipe", 1)
    values, branch = layer_terms(
        arrived, gain_row, w_gate, w_up, down_all, route_ids[0, 1], route_wts[0, 1]
    )
    second = (values + branch).astype(jnp.bfloat16)
    result_rows = jnp.where(section_index == 0, arrived, second)
    return result_rows[None]


def solution(mesh):
    n_x = EXPERTS
    n_pipe, n_expert = mesh.devices.shape
    split_mesh = Mesh(
        mesh.devices.reshape(n_pipe, n_x, n_expert // n_x), ("pipe", "ex", "ey")
    )
    rows = ("ex", "ey")
    return jax.shard_map(
        shards,
        mesh=split_mesh,
        in_specs=(
            P("pipe", rows, None),
            P("pipe", None),
            P("pipe", rows, None, None),
            P("pipe", rows, None, None),
            P("pipe", rows, None, None),
            P("pipe", None, rows, None),
            P("pipe", None, rows, None),
        ),
        out_specs=P("pipe", rows, None),
        check_vma=False,
    )
```

```python
import jax
import jax.numpy as jnp
from jax import lax
from jax.sharding import Mesh
from jax.sharding import PartitionSpec as P

EXPERTS = 4
MOST = 17
LANE = 128


NORM_EPS = 1e-06
FIXED_UNIT = 1.0 / 4096.0


def shifted(value, axis, steps):
    count = lax.axis_size(axis)
    pairs = [(source, (source + steps) % count) for source in range(count)]
    return lax.ppermute(value, axis, pairs)


def slot_index(expert_ids, capacity, experts):
    flat_ids = expert_ids.reshape(-1)
    onehot = (flat_ids[:, None] == jnp.arange(experts, dtype=jnp.int32)[None, :]).astype(jnp.int32)
    before = jnp.cumsum(onehot, axis=0) - onehot
    slot_rank = jnp.sum(before * onehot, axis=1)
    return (flat_ids * capacity + slot_rank).reshape(expert_ids.shape)


def place_rows(normed, slot_ids, slot_total):
    slot_marks = slot_ids[:, :, None] == jnp.arange(slot_total, dtype=jnp.int32)[None, None, :]
    placing = jnp.sum(slot_marks.astype(jnp.float32), axis=1).T.astype(jnp.bfloat16)
    return jnp.dot(placing, normed, preferred_element_type=jnp.float32).astype(jnp.bfloat16)


def routed_branch(normed, expert_ids, route_weight, w_gate, w_up, down_all):
    n_x = lax.axis_size("ex")
    model_width = normed.shape[1]
    slot_ids = slot_index(expert_ids, MOST, EXPERTS)
    block_rows = MOST * model_width // LANE
    per_expert = place_rows(normed, slot_ids, EXPERTS * MOST).reshape(EXPERTS, block_rows, LANE)
    from_x = lax.all_to_all(per_expert, "ex", split_axis=0, concat_axis=0, tiled=True)
    slot_rows = lax.all_gather(from_x, "ey", axis=0, tiled=False)
    n_y = slot_rows.shape[0]
    flat_rows = slot_rows.reshape(-1, model_width)
    gate_act = jnp.dot(flat_rows, w_gate, preferred_element_type=jnp.float32)
    up_act = jnp.dot(flat_rows, w_up, preferred_element_type=jnp.float32)
    hidden = (jax.nn.silu(gate_act) * up_act).astype(jnp.bfloat16)
    hidden = hidden.reshape(n_y, n_x * MOST, hidden.shape[-1])
    hidden_here = lax.all_to_all(hidden, "ey", split_axis=0, concat_axis=0, tiled=True)
    parts = jnp.einsum("jrh,jhd->jrd", hidden_here, down_all, preferred_element_type=jnp.float32)
    expert_out = jnp.sum(parts.astype(jnp.bfloat16).astype(jnp.float32), axis=0)
    expert_out = expert_out.reshape(n_x, block_rows, LANE)
    returned = lax.all_to_all(expert_out, "ex", split_axis=0, concat_axis=0, tiled=True)
    picked = returned.reshape(EXPERTS * MOST, model_width)[slot_ids]
    weights = route_weight.astype(jnp.float32) * FIXED_UNIT
    return jnp.sum(weights[:, :, None] * picked, axis=1)


def layer_terms(rows_in, gain_row, w_gate, w_up, down_all, expert_ids, route_weight):
    values = rows_in.astype(jnp.float32)
    inv_rms = lax.rsqrt(jnp.mean(values * values, axis=1, keepdims=True) + NORM_EPS)
    normed = (values * inv_rms * gain_row.astype(jnp.float32)).astype(jnp.bfloat16)
    branch = routed_branch(normed, expert_ids, route_weight, w_gate, w_up, down_all)
    return (values, branch)


def shards(acts, norm_gain, gate_w, up_w, down_w, route_ids, route_wts):
    section_index = lax.axis_index("pipe")
    rows_in = acts[0]
    gain_row = norm_gain[0]
    w_gate = gate_w[0, 0]
    w_up = up_w[0, 0]
    down_all = lax.all_gather(down_w[0, 0], "ey", axis=0, tiled=False)
    values, branch = layer_terms(
        rows_in, gain_row, w_gate, w_up, down_all, route_ids[0, 0], route_wts[0, 0]
    )
    first_out = (values + branch).astype(jnp.bfloat16)
    arrived = shifted(first_out, "pipe", 1)
    values, branch = layer_terms(
        arrived, gain_row, w_gate, w_up, down_all, route_ids[0, 1], route_wts[0, 1]
    )
    second = (values + branch).astype(jnp.bfloat16)
    result_rows = jnp.where(section_index == 0, arrived, second)
    return result_rows[None]


def solution(mesh):
    n_x = EXPERTS
    n_pipe, n_expert = mesh.devices.shape
    split_mesh = Mesh(
        mesh.devices.reshape(n_pipe, n_x, n_expert // n_x), ("pipe", "ex", "ey")
    )
    rows = ("ex", "ey")
    return jax.shard_map(
        shards,
        mesh=split_mesh,
        in_specs=(
            P("pipe", rows, None),
            P("pipe", None),
            P("pipe", rows, None, None),
            P("pipe", rows, None, None),
            P("pipe", rows, None, None),
            P("pipe", None, rows, None),
            P("pipe", None, rows, None),
        ),
        out_specs=P("pipe", rows, None),
        check_vma=False,
    )
```

```python
import jax
import jax.numpy as jnp
from jax import lax
from jax.sharding import Mesh
from jax.sharding import PartitionSpec as P

EXPERTS = 4
MOST = 17
LANE = 128


NORM_EPS = 1e-06
FIXED_UNIT = 1.0 / 4096.0


def shifted(value, axis, steps):
    count = lax.axis_size(axis)
    pairs = [(source, (source + steps) % count) for source in range(count)]
    return lax.ppermute(value, axis, pairs)


def next_section_shift(value, steps):
    n_pipe = lax.axis_size("pipe")
    n_x = lax.axis_size("ex")
    pairs = []
    for p in range(n_pipe):
        for x in range(n_x):
            pairs.append((p * n_x + x, ((p + 1) % n_pipe) * n_x + (x + steps) % n_x))
    return lax.ppermute(value, ("pipe", "ex"), pairs)


def slot_index(expert_ids, me_x):
    flat_ids = expert_ids.reshape(-1)
    relative = (flat_ids - me_x) % EXPERTS
    onehot = (relative[:, None] == jnp.arange(EXPERTS, dtype=jnp.int32)[None, :]).astype(jnp.int32)
    before = jnp.cumsum(onehot, axis=0) - onehot
    slot_rank = jnp.sum(before * onehot, axis=1)
    return (relative * MOST + slot_rank).reshape(expert_ids.shape)


def place_rows(normed, slot_ids, slot_total):
    slot_marks = slot_ids[:, :, None] == jnp.arange(slot_total, dtype=jnp.int32)[None, None, :]
    placing = jnp.sum(slot_marks.astype(jnp.float32), axis=1).T.astype(jnp.bfloat16)
    return jnp.dot(placing, normed, preferred_element_type=jnp.float32).astype(jnp.bfloat16)


def normalize(rows_in, gain_row):
    values = rows_in.astype(jnp.float32)
    inv_rms = lax.rsqrt(jnp.mean(values * values, axis=1, keepdims=True) + NORM_EPS)
    normed = (values * inv_rms * gain_row.astype(jnp.float32)).astype(jnp.bfloat16)
    return values, normed


def slot_blocks(normed, slot_ids):
    model_width = normed.shape[1]
    placed = place_rows(normed, slot_ids, EXPERTS * MOST)
    return placed.reshape(EXPERTS, MOST * model_width // LANE, LANE)


def serve(from_x, w_gate, w_up, down_all):
    n_x = from_x.shape[0]
    model_width = w_gate.shape[0]
    me_y = lax.axis_index("ey")
    slot_rows = lax.all_gather(from_x, "ey", axis=0, tiled=False)
    n_y = slot_rows.shape[0]
    flat_rows = slot_rows.reshape(-1, model_width)
    gate_act = jnp.dot(flat_rows, w_gate, preferred_element_type=jnp.float32)
    up_act = jnp.dot(flat_rows, w_up, preferred_element_type=jnp.float32)
    hidden = (jax.nn.silu(gate_act) * up_act).astype(jnp.bfloat16)
    hidden = hidden.reshape(n_y, n_x * MOST, hidden.shape[-1])
    received = [hidden[me_y][None]]
    for d in range(1, n_y):
        piece = lax.dynamic_index_in_dim(hidden, (me_y + d) % n_y, 0, keepdims=True)
        received.append(shifted(piece, "ey", d))
    received = jnp.concatenate(received, axis=0)
    hidden_here = jnp.take(received, (me_y - jnp.arange(n_y)) % n_y, axis=0)
    parts = jnp.einsum("jrh,jhd->jrd", hidden_here, down_all, preferred_element_type=jnp.float32)
    expert_out = jnp.sum(parts.astype(jnp.bfloat16).astype(jnp.float32), axis=0)
    expert_out = expert_out.reshape(n_x, MOST * model_width // LANE, LANE)
    back = [expert_out[0]]
    for d in range(1, n_x):
        back.append(shifted(expert_out[d], "ex", -d))
    return jnp.stack(back, axis=0)


def finish(values, returned, slot_ids, route_weight):
    model_width = values.shape[1]
    picked = returned.reshape(EXPERTS * MOST, model_width)[slot_ids]
    weights = route_weight.astype(jnp.float32) * FIXED_UNIT
    branch = jnp.sum(weights[:, :, None] * picked, axis=1)
    return (values + branch).astype(jnp.bfloat16)


def shards(acts, norm_gain, gate_w, up_w, down_w, route_ids, route_wts):
    section_index = lax.axis_index("pipe")
    me_x = lax.axis_index("ex")
    rows_in = acts[0]
    gain_row = norm_gain[0]
    w_gate = gate_w[0, 0]
    w_up = up_w[0, 0]
    down_all = lax.all_gather(down_w[0, 0], "ey", axis=0, tiled=False)
    gain_next = shifted(gain_row, "pipe", -1)
    ids_next = shifted(route_ids[0, 1], "pipe", -1)

    values, normed = normalize(rows_in, gain_row)
    slot_ids = slot_index(route_ids[0, 0], me_x)
    blocks = slot_blocks(normed, slot_ids)
    from_x = [blocks[0]]
    for d in range(1, EXPERTS):
        from_x.append(shifted(blocks[d], "ex", d))
    returned = serve(jnp.stack(from_x, axis=0), w_gate, w_up, down_all)
    first_out = finish(values, returned, slot_ids, route_wts[0, 0])

    arrived = shifted(first_out, "pipe", 1)
    _, normed_next = normalize(first_out, gain_next)
    blocks_next = slot_blocks(normed_next, slot_index(ids_next, me_x))
    from_x = [next_section_shift(blocks_next[d], d) for d in range(EXPERTS)]
    returned = serve(jnp.stack(from_x, axis=0), w_gate, w_up, down_all)
    slot_ids = slot_index(route_ids[0, 1], me_x)
    second = finish(arrived.astype(jnp.float32), returned, slot_ids, route_wts[0, 1])

    result_rows = jnp.where(section_index == 0, arrived, second)
    return result_rows[None]


def solution(mesh):
    n_x = EXPERTS
    n_pipe, n_expert = mesh.devices.shape
    split_mesh = Mesh(
        mesh.devices.reshape(n_pipe, n_x, n_expert // n_x), ("pipe", "ex", "ey")
    )
    rows = ("ex", "ey")
    return jax.shard_map(
        shards,
        mesh=split_mesh,
        in_specs=(
            P("pipe", rows, None),
            P("pipe", None),
            P("pipe", rows, None, None),
            P("pipe", rows, None, None),
            P("pipe", rows, None, None),
            P("pipe", None, rows, None),
            P("pipe", None, rows, None),
        ),
        out_specs=P("pipe", rows, None),
        check_vma=False,
    )
```

```python
import jax
import jax.numpy as jnp
from jax import lax
from jax.sharding import Mesh
from jax.sharding import PartitionSpec as P

EXPERTS = 4
MOST = 17
LANE = 128


NORM_EPS = 1e-06
FIXED_UNIT = 1.0 / 4096.0


def shifted(value, axis, steps):
    count = lax.axis_size(axis)
    pairs = [(source, (source + steps) % count) for source in range(count)]
    return lax.ppermute(value, axis, pairs)


def slot_index(expert_ids, capacity, experts):
    flat_ids = expert_ids.reshape(-1)
    onehot = (flat_ids[:, None] == jnp.arange(experts, dtype=jnp.int32)[None, :]).astype(jnp.int32)
    before = jnp.cumsum(onehot, axis=0) - onehot
    slot_rank = jnp.sum(before * onehot, axis=1)
    return (flat_ids * capacity + slot_rank).reshape(expert_ids.shape)


def place_rows(normed, slot_ids, slot_total):
    slot_marks = slot_ids[:, :, None] == jnp.arange(slot_total, dtype=jnp.int32)[None, None, :]
    placing = jnp.sum(slot_marks.astype(jnp.float32), axis=1).T.astype(jnp.bfloat16)
    return jnp.dot(placing, normed, preferred_element_type=jnp.float32).astype(jnp.bfloat16)


def routed_branch(normed, expert_ids, route_weight, w_gate, w_up, down_all, down_first=None):
    n_x = lax.axis_size("ex")
    model_width = normed.shape[1]
    slot_ids = slot_index(expert_ids, MOST, EXPERTS)
    block_rows = MOST * model_width // LANE
    per_expert = place_rows(normed, slot_ids, EXPERTS * MOST).reshape(EXPERTS, block_rows, LANE)
    from_x = lax.all_to_all(per_expert, "ex", split_axis=0, concat_axis=0, tiled=True)
    if down_first is not None:
        from_x, down_first = lax.optimization_barrier((from_x, down_first))
    slot_rows = lax.all_gather(from_x, "ey", axis=0, tiled=False)
    if callable(down_all):
        slot_rows, down_all = down_all(slot_rows, down_first)
    n_y = slot_rows.shape[0]
    flat_rows = slot_rows.reshape(-1, model_width)
    gate_act = jnp.dot(flat_rows, w_gate, preferred_element_type=jnp.float32)
    up_act = jnp.dot(flat_rows, w_up, preferred_element_type=jnp.float32)
    hidden = (jax.nn.silu(gate_act) * up_act).astype(jnp.bfloat16)
    hidden = hidden.reshape(n_y, n_x * MOST, hidden.shape[-1])
    hidden_here = lax.all_to_all(hidden, "ey", split_axis=0, concat_axis=0, tiled=True)
    if isinstance(down_all, tuple):
        split = down_all[0].shape[1]
        parts = jnp.einsum("jrh,jhd->jrd", hidden_here[:, :, :split], down_all[0], preferred_element_type=jnp.float32)
        parts = parts + jnp.einsum("jrh,jhd->jrd", hidden_here[:, :, split:], down_all[1], preferred_element_type=jnp.float32)
    else:
        parts = jnp.einsum("jrh,jhd->jrd", hidden_here, down_all, preferred_element_type=jnp.float32)
    expert_out = jnp.sum(parts.astype(jnp.bfloat16).astype(jnp.float32), axis=0)
    expert_out = expert_out.reshape(n_x, block_rows, LANE)
    returned = lax.all_to_all(expert_out, "ex", split_axis=0, concat_axis=0, tiled=True)
    picked = returned.reshape(EXPERTS * MOST, model_width)[slot_ids]
    weights = route_weight.astype(jnp.float32) * FIXED_UNIT
    return jnp.sum(weights[:, :, None] * picked, axis=1)


def layer_terms(rows_in, gain_row, w_gate, w_up, down_all, expert_ids, route_weight, down_first=None):
    values = rows_in.astype(jnp.float32)
    inv_rms = lax.rsqrt(jnp.mean(values * values, axis=1, keepdims=True) + NORM_EPS)
    normed = (values * inv_rms * gain_row.astype(jnp.float32)).astype(jnp.bfloat16)
    branch = routed_branch(normed, expert_ids, route_weight, w_gate, w_up, down_all, down_first)
    return (values, branch)


def shards(acts, norm_gain, gate_w, up_w, down_w, route_ids, route_wts):
    section_index = lax.axis_index("pipe")
    rows_in = acts[0]
    gain_row = norm_gain[0]
    w_gate = gate_w[0, 0]
    w_up = up_w[0, 0]
    split = down_w.shape[2] // 4
    down_first = lax.all_gather(down_w[0, 0, :split], "ey", axis=0, tiled=False)
    gathered = []

    def down_rest(slot_rows, first_part):
        slot_rows, rest = lax.optimization_barrier((slot_rows, down_w[0, 0, split:]))
        gathered.append((first_part, lax.all_gather(rest, "ey", axis=0, tiled=False)))
        return slot_rows, gathered[0]

    values, branch = layer_terms(
        rows_in, gain_row, w_gate, w_up, down_rest, route_ids[0, 0], route_wts[0, 0], down_first
    )
    down_all = gathered[0]
    first_out = (values + branch).astype(jnp.bfloat16)
    arrived = shifted(first_out, "pipe", 1)
    values, branch = layer_terms(
        arrived, gain_row, w_gate, w_up, down_all, route_ids[0, 1], route_wts[0, 1]
    )
    second = (values + branch).astype(jnp.bfloat16)
    result_rows = jnp.where(section_index == 0, arrived, second)
    return result_rows[None]


def solution(mesh):
    n_x = EXPERTS
    n_pipe, n_expert = mesh.devices.shape
    split_mesh = Mesh(
        mesh.devices.reshape(n_pipe, n_x, n_expert // n_x), ("pipe", "ex", "ey")
    )
    rows = ("ex", "ey")
    return jax.shard_map(
        shards,
        mesh=split_mesh,
        in_specs=(
            P("pipe", rows, None),
            P("pipe", None),
            P("pipe", rows, None, None),
            P("pipe", rows, None, None),
            P("pipe", rows, None, None),
            P("pipe", None, rows, None),
            P("pipe", None, rows, None),
        ),
        out_specs=P("pipe", rows, None),
        check_vma=False,
    )
```

```python
import jax
import jax.numpy as jnp
from jax import lax
from jax.sharding import Mesh
from jax.sharding import PartitionSpec as P

EXPERTS = 4
MOST = 17
LANE = 128


NORM_EPS = 1e-06
FIXED_UNIT = 1.0 / 4096.0


def shifted(value, axis, steps):
    count = lax.axis_size(axis)
    pairs = [(source, (source + steps) % count) for source in range(count)]
    return lax.ppermute(value, axis, pairs)


def ring_gather(value, axis):
    count = lax.axis_size(axis)
    ahead, behind = {0: value}, {}
    forward, backward = value, value
    for step in range(1, count // 2 + 1):
        forward = shifted(forward, axis, 1)
        behind[step] = forward
        if step < count - step:
            backward = shifted(backward, axis, -1)
            ahead[step] = backward
    return [ahead[d] if d in ahead else behind[count - d] for d in range(count)]


def slot_index(expert_ids, capacity, experts):
    flat_ids = expert_ids.reshape(-1)
    onehot = (flat_ids[:, None] == jnp.arange(experts, dtype=jnp.int32)[None, :]).astype(jnp.int32)
    before = jnp.cumsum(onehot, axis=0) - onehot
    slot_rank = jnp.sum(before * onehot, axis=1)
    return (flat_ids * capacity + slot_rank).reshape(expert_ids.shape)


def place_rows(normed, slot_ids, slot_total):
    slot_marks = slot_ids[:, :, None] == jnp.arange(slot_total, dtype=jnp.int32)[None, None, :]
    placing = jnp.sum(slot_marks.astype(jnp.float32), axis=1).T.astype(jnp.bfloat16)
    return jnp.dot(placing, normed, preferred_element_type=jnp.float32).astype(jnp.bfloat16)


def routed_branch(normed, expert_ids, route_weight, w_gate, w_up, down_all):
    n_x = lax.axis_size("ex")
    model_width = normed.shape[1]
    slot_ids = slot_index(expert_ids, MOST, EXPERTS)
    block_rows = MOST * model_width // LANE
    per_expert = place_rows(normed, slot_ids, EXPERTS * MOST).reshape(EXPERTS, block_rows, LANE)
    from_x = lax.all_to_all(per_expert, "ex", split_axis=0, concat_axis=0, tiled=True)
    slot_rows = lax.all_gather(from_x, "ey", axis=0, tiled=False)
    n_y = slot_rows.shape[0]
    flat_rows = slot_rows.reshape(-1, model_width)
    gate_act = jnp.dot(flat_rows, w_gate, preferred_element_type=jnp.float32)
    up_act = jnp.dot(flat_rows, w_up, preferred_element_type=jnp.float32)
    hidden = (jax.nn.silu(gate_act) * up_act).astype(jnp.bfloat16)
    hidden = hidden.reshape(n_y, n_x * MOST, hidden.shape[-1])
    hidden_here = lax.all_to_all(hidden, "ey", split_axis=0, concat_axis=0, tiled=True)
    me_y = lax.axis_index("ey")
    hidden_rel = jnp.take(hidden_here, (me_y + jnp.arange(n_y)) % n_y, axis=0)
    expert_out = None
    for d in range(n_y):
        part = jnp.dot(hidden_rel[d], down_all[d], preferred_element_type=jnp.float32)
        part = part.astype(jnp.bfloat16).astype(jnp.float32)
        expert_out = part if expert_out is None else expert_out + part
    expert_out = expert_out.reshape(n_x, block_rows, LANE)
    returned = lax.all_to_all(expert_out, "ex", split_axis=0, concat_axis=0, tiled=True)
    picked = returned.reshape(EXPERTS * MOST, model_width)[slot_ids]
    weights = route_weight.astype(jnp.float32) * FIXED_UNIT
    return jnp.sum(weights[:, :, None] * picked, axis=1)


def layer_terms(rows_in, gain_row, w_gate, w_up, down_all, expert_ids, route_weight):
    values = rows_in.astype(jnp.float32)
    inv_rms = lax.rsqrt(jnp.mean(values * values, axis=1, keepdims=True) + NORM_EPS)
    normed = (values * inv_rms * gain_row.astype(jnp.float32)).astype(jnp.bfloat16)
    branch = routed_branch(normed, expert_ids, route_weight, w_gate, w_up, down_all)
    return (values, branch)


def shards(acts, norm_gain, gate_w, up_w, down_w, route_ids, route_wts):
    section_index = lax.axis_index("pipe")
    rows_in = acts[0]
    gain_row = norm_gain[0]
    w_gate = gate_w[0, 0]
    w_up = up_w[0, 0]
    down_all = ring_gather(down_w[0, 0], "ey")
    values, branch = layer_terms(
        rows_in, gain_row, w_gate, w_up, down_all, route_ids[0, 0], route_wts[0, 0]
    )
    first_out = (values + branch).astype(jnp.bfloat16)
    arrived = shifted(first_out, "pipe", 1)
    values, branch = layer_terms(
        arrived, gain_row, w_gate, w_up, down_all, route_ids[0, 1], route_wts[0, 1]
    )
    second = (values + branch).astype(jnp.bfloat16)
    result_rows = jnp.where(section_index == 0, arrived, second)
    return result_rows[None]


def solution(mesh):
    n_x = EXPERTS
    n_pipe, n_expert = mesh.devices.shape
    split_mesh = Mesh(
        mesh.devices.reshape(n_pipe, n_x, n_expert // n_x), ("pipe", "ex", "ey")
    )
    rows = ("ex", "ey")
    return jax.shard_map(
        shards,
        mesh=split_mesh,
        in_specs=(
            P("pipe", rows, None),
            P("pipe", None),
            P("pipe", rows, None, None),
            P("pipe", rows, None, None),
            P("pipe", rows, None, None),
            P("pipe", None, rows, None),
            P("pipe", None, rows, None),
        ),
        out_specs=P("pipe", rows, None),
        check_vma=False,
    )
```

```python
import jax
import jax.numpy as jnp
from jax import lax
from jax.sharding import Mesh
from jax.sharding import PartitionSpec as P

EXPERTS = 4
MOST = 17
LANE = 128


NORM_EPS = 1e-06
FIXED_UNIT = 1.0 / 4096.0


def shifted(value, axis, steps):
    count = lax.axis_size(axis)
    pairs = [(source, (source + steps) % count) for source in range(count)]
    return lax.ppermute(value, axis, pairs)


def ring_gather(value, axis):
    count = lax.axis_size(axis)
    ahead, behind = {0: value}, {}
    forward, backward = value, value
    for step in range(1, (count + 1) // 2):
        forward = shifted(forward, axis, 1)
        behind[step] = forward
        backward = shifted(backward, axis, -1)
        ahead[step] = backward
    if count % 2 == 0:
        half = value.shape[0] // 2
        ahead[count // 2] = jnp.concatenate(
            [shifted(forward[:half], axis, 1), shifted(backward[half:], axis, -1)], axis=0
        )
    return [ahead[d] if d in ahead else behind[count - d] for d in range(count)]


def slot_index(expert_ids, capacity, experts):
    flat_ids = expert_ids.reshape(-1)
    onehot = (flat_ids[:, None] == jnp.arange(experts, dtype=jnp.int32)[None, :]).astype(jnp.int32)
    before = jnp.cumsum(onehot, axis=0) - onehot
    slot_rank = jnp.sum(before * onehot, axis=1)
    return (flat_ids * capacity + slot_rank).reshape(expert_ids.shape)


def place_rows(normed, slot_ids, slot_total):
    slot_marks = slot_ids[:, :, None] == jnp.arange(slot_total, dtype=jnp.int32)[None, None, :]
    placing = jnp.sum(slot_marks.astype(jnp.float32), axis=1).T.astype(jnp.bfloat16)
    return jnp.dot(placing, normed, preferred_element_type=jnp.float32).astype(jnp.bfloat16)


def routed_branch(normed, expert_ids, route_weight, w_gate, w_up, down_all):
    n_x = lax.axis_size("ex")
    model_width = normed.shape[1]
    slot_ids = slot_index(expert_ids, MOST, EXPERTS)
    block_rows = MOST * model_width // LANE
    per_expert = place_rows(normed, slot_ids, EXPERTS * MOST).reshape(EXPERTS, block_rows, LANE)
    from_x = lax.all_to_all(per_expert, "ex", split_axis=0, concat_axis=0, tiled=True)
    slot_rows = lax.all_gather(from_x, "ey", axis=0, tiled=False)
    n_y = slot_rows.shape[0]
    flat_rows = slot_rows.reshape(-1, model_width)
    gate_act = jnp.dot(flat_rows, w_gate, preferred_element_type=jnp.float32)
    up_act = jnp.dot(flat_rows, w_up, preferred_element_type=jnp.float32)
    hidden = (jax.nn.silu(gate_act) * up_act).astype(jnp.bfloat16)
    hidden = hidden.reshape(n_y, n_x * MOST, hidden.shape[-1])
    hidden_here = lax.all_to_all(hidden, "ey", split_axis=0, concat_axis=0, tiled=True)
    me_y = lax.axis_index("ey")
    hidden_rel = jnp.take(hidden_here, (me_y + jnp.arange(n_y)) % n_y, axis=0)
    if isinstance(down_all, list):
        expert_out = None
        for d in range(n_y):
            part = jnp.dot(hidden_rel[d], down_all[d], preferred_element_type=jnp.float32)
            part = part.astype(jnp.bfloat16).astype(jnp.float32)
            expert_out = part if expert_out is None else expert_out + part
    else:
        parts = jnp.einsum("jrh,jhd->jrd", hidden_rel, down_all, preferred_element_type=jnp.float32)
        expert_out = jnp.sum(parts.astype(jnp.bfloat16).astype(jnp.float32), axis=0)
    expert_out = expert_out.reshape(n_x, block_rows, LANE)
    returned = lax.all_to_all(expert_out, "ex", split_axis=0, concat_axis=0, tiled=True)
    picked = returned.reshape(EXPERTS * MOST, model_width)[slot_ids]
    weights = route_weight.astype(jnp.float32) * FIXED_UNIT
    return jnp.sum(weights[:, :, None] * picked, axis=1)


def layer_terms(rows_in, gain_row, w_gate, w_up, down_all, expert_ids, route_weight):
    values = rows_in.astype(jnp.float32)
    inv_rms = lax.rsqrt(jnp.mean(values * values, axis=1, keepdims=True) + NORM_EPS)
    normed = (values * inv_rms * gain_row.astype(jnp.float32)).astype(jnp.bfloat16)
    branch = routed_branch(normed, expert_ids, route_weight, w_gate, w_up, down_all)
    return (values, branch)


def shards(acts, norm_gain, gate_w, up_w, down_w, route_ids, route_wts):
    section_index = lax.axis_index("pipe")
    rows_in = acts[0]
    gain_row = norm_gain[0]
    w_gate = gate_w[0, 0]
    w_up = up_w[0, 0]
    down_all = ring_gather(down_w[0, 0], "ey")
    values, branch = layer_terms(
        rows_in, gain_row, w_gate, w_up, down_all, route_ids[0, 0], route_wts[0, 0]
    )
    first_out = (values + branch).astype(jnp.bfloat16)
    arrived = shifted(first_out, "pipe", 1)
    values, branch = layer_terms(
        arrived, gain_row, w_gate, w_up, jnp.stack(down_all, axis=0), route_ids[0, 1], route_wts[0, 1]
    )
    second = (values + branch).astype(jnp.bfloat16)
    result_rows = jnp.where(section_index == 0, arrived, second)
    return result_rows[None]


def solution(mesh):
    n_x = EXPERTS
    n_pipe, n_expert = mesh.devices.shape
    split_mesh = Mesh(
        mesh.devices.reshape(n_pipe, n_x, n_expert // n_x), ("pipe", "ex", "ey")
    )
    rows = ("ex", "ey")
    return jax.shard_map(
        shards,
        mesh=split_mesh,
        in_specs=(
            P("pipe", rows, None),
            P("pipe", None),
            P("pipe", rows, None, None),
            P("pipe", rows, None, None),
            P("pipe", rows, None, None),
            P("pipe", None, rows, None),
            P("pipe", None, rows, None),
        ),
        out_specs=P("pipe", rows, None),
        check_vma=False,
    )
```

```python
import jax
import jax.numpy as jnp
from jax import lax
from jax.sharding import Mesh
from jax.sharding import PartitionSpec as P

EXPERTS = 4
MOST = 17
LANE = 128


NORM_EPS = 1e-06
FIXED_UNIT = 1.0 / 4096.0


def shifted(value, axis, steps):
    count = lax.axis_size(axis)
    pairs = [(source, (source + steps) % count) for source in range(count)]
    return lax.ppermute(value, axis, pairs)


def ring_gather(value, axis, first_hop=None):
    count = lax.axis_size(axis)
    ahead, behind = {0: value}, {}
    forward, backward = value, value
    start = 1
    if first_hop is not None:
        forward, backward = first_hop
        behind[1], ahead[1] = forward, backward
        start = 2
    for step in range(start, count // 2 + 1):
        forward = shifted(forward, axis, 1)
        behind[step] = forward
        if step < count - step:
            backward = shifted(backward, axis, -1)
            ahead[step] = backward
    return [ahead[d] if d in ahead else behind[count - d] for d in range(count)]


def slot_index(expert_ids, capacity, experts):
    flat_ids = expert_ids.reshape(-1)
    onehot = (flat_ids[:, None] == jnp.arange(experts, dtype=jnp.int32)[None, :]).astype(jnp.int32)
    before = jnp.cumsum(onehot, axis=0) - onehot
    slot_rank = jnp.sum(before * onehot, axis=1)
    return (flat_ids * capacity + slot_rank).reshape(expert_ids.shape)


def place_rows(normed, slot_ids, slot_total):
    slot_marks = slot_ids[:, :, None] == jnp.arange(slot_total, dtype=jnp.int32)[None, None, :]
    placing = jnp.sum(slot_marks.astype(jnp.float32), axis=1).T.astype(jnp.bfloat16)
    return jnp.dot(placing, normed, preferred_element_type=jnp.float32).astype(jnp.bfloat16)


def routed_branch(normed, expert_ids, route_weight, w_gate, w_up, down_all, before_x=None):
    n_x = lax.axis_size("ex")
    model_width = normed.shape[1]
    slot_ids = slot_index(expert_ids, MOST, EXPERTS)
    block_rows = MOST * model_width // LANE
    per_expert = place_rows(normed, slot_ids, EXPERTS * MOST).reshape(EXPERTS, block_rows, LANE)
    if before_x is not None:
        per_expert, down_all = before_x(per_expert)
    from_x = lax.all_to_all(per_expert, "ex", split_axis=0, concat_axis=0, tiled=True)
    slot_rows = lax.all_gather(from_x, "ey", axis=0, tiled=False)
    n_y = slot_rows.shape[0]
    flat_rows = slot_rows.reshape(-1, model_width)
    gate_act = jnp.dot(flat_rows, w_gate, preferred_element_type=jnp.float32)
    up_act = jnp.dot(flat_rows, w_up, preferred_element_type=jnp.float32)
    hidden = (jax.nn.silu(gate_act) * up_act).astype(jnp.bfloat16)
    hidden = hidden.reshape(n_y, n_x * MOST, hidden.shape[-1])
    hidden_here = lax.all_to_all(hidden, "ey", split_axis=0, concat_axis=0, tiled=True)
    me_y = lax.axis_index("ey")
    hidden_rel = jnp.take(hidden_here, (me_y + jnp.arange(n_y)) % n_y, axis=0)
    expert_out = None
    for d in range(n_y):
        part = jnp.dot(hidden_rel[d], down_all[d], preferred_element_type=jnp.float32)
        part = part.astype(jnp.bfloat16).astype(jnp.float32)
        expert_out = part if expert_out is None else expert_out + part
    expert_out = expert_out.reshape(n_x, block_rows, LANE)
    returned = lax.all_to_all(expert_out, "ex", split_axis=0, concat_axis=0, tiled=True)
    picked = returned.reshape(EXPERTS * MOST, model_width)[slot_ids]
    weights = route_weight.astype(jnp.float32) * FIXED_UNIT
    return jnp.sum(weights[:, :, None] * picked, axis=1)


def layer_terms(rows_in, gain_row, w_gate, w_up, down_all, expert_ids, route_weight, before_x=None):
    values = rows_in.astype(jnp.float32)
    inv_rms = lax.rsqrt(jnp.mean(values * values, axis=1, keepdims=True) + NORM_EPS)
    normed = (values * inv_rms * gain_row.astype(jnp.float32)).astype(jnp.bfloat16)
    branch = routed_branch(normed, expert_ids, route_weight, w_gate, w_up, down_all, before_x)
    return (values, branch)


def shards(acts, norm_gain, gate_w, up_w, down_w, route_ids, route_wts):
    section_index = lax.axis_index("pipe")
    rows_in = acts[0]
    gain_row = norm_gain[0]
    w_gate = gate_w[0, 0]
    w_up = up_w[0, 0]
    own_down = down_w[0, 0]
    first_hop = (shifted(own_down, "ey", 1), shifted(own_down, "ey", -1))
    gathered = []

    def before_x(per_expert):
        per_expert, hop = lax.optimization_barrier((per_expert, first_hop))
        gathered.append(ring_gather(own_down, "ey", hop))
        return per_expert, gathered[0]

    values, branch = layer_terms(
        rows_in, gain_row, w_gate, w_up, None, route_ids[0, 0], route_wts[0, 0], before_x
    )
    down_all = gathered[0]
    first_out = (values + branch).astype(jnp.bfloat16)
    arrived = shifted(first_out, "pipe", 1)
    values, branch = layer_terms(
        arrived, gain_row, w_gate, w_up, down_all, route_ids[0, 1], route_wts[0, 1]
    )
    second = (values + branch).astype(jnp.bfloat16)
    result_rows = jnp.where(section_index == 0, arrived, second)
    return result_rows[None]


def solution(mesh):
    n_x = EXPERTS
    n_pipe, n_expert = mesh.devices.shape
    split_mesh = Mesh(
        mesh.devices.reshape(n_pipe, n_x, n_expert // n_x), ("pipe", "ex", "ey")
    )
    rows = ("ex", "ey")
    return jax.shard_map(
        shards,
        mesh=split_mesh,
        in_specs=(
            P("pipe", rows, None),
            P("pipe", None),
            P("pipe", rows, None, None),
            P("pipe", rows, None, None),
            P("pipe", rows, None, None),
            P("pipe", None, rows, None),
            P("pipe", None, rows, None),
        ),
        out_specs=P("pipe", rows, None),
        check_vma=False,
    )
```

```python
import jax
import jax.numpy as jnp
from jax import lax
from jax.sharding import Mesh
from jax.sharding import PartitionSpec as P

EXPERTS = 4
MOST = 17
LANE = 128


NORM_EPS = 1e-06
FIXED_UNIT = 1.0 / 4096.0


def shifted(value, axis, steps):
    count = lax.axis_size(axis)
    pairs = [(source, (source + steps) % count) for source in range(count)]
    return lax.ppermute(value, axis, pairs)


def ring_gather(value, axis):
    count = lax.axis_size(axis)
    ahead, behind = {0: value}, {}
    forward, backward = value, value
    for step in range(1, count // 2 + 1):
        forward = shifted(forward, axis, 1)
        behind[step] = forward
        if step < count - step:
            backward = shifted(backward, axis, -1)
            ahead[step] = backward
    return [ahead[d] if d in ahead else behind[count - d] for d in range(count)]


def slot_index(expert_ids, capacity, experts):
    flat_ids = expert_ids.reshape(-1)
    onehot = (flat_ids[:, None] == jnp.arange(experts, dtype=jnp.int32)[None, :]).astype(jnp.int32)
    before = jnp.cumsum(onehot, axis=0) - onehot
    slot_rank = jnp.sum(before * onehot, axis=1)
    return (flat_ids * capacity + slot_rank).reshape(expert_ids.shape)


def place_rows(normed, slot_ids, slot_total):
    slot_marks = slot_ids[:, :, None] == jnp.arange(slot_total, dtype=jnp.int32)[None, None, :]
    placing = jnp.sum(slot_marks.astype(jnp.float32), axis=1).T.astype(jnp.bfloat16)
    return jnp.dot(placing, normed, preferred_element_type=jnp.float32).astype(jnp.bfloat16)


def routed_branch(normed, expert_ids, route_weight, w_gate, w_up, down_all):
    n_x = lax.axis_size("ex")
    model_width = normed.shape[1]
    slot_ids = slot_index(expert_ids, MOST, EXPERTS)
    block_rows = MOST * model_width // LANE
    per_expert = place_rows(normed, slot_ids, EXPERTS * MOST).reshape(EXPERTS, block_rows, LANE)
    from_x = lax.all_to_all(per_expert, "ex", split_axis=0, concat_axis=0, tiled=True)
    slot_rows = lax.all_gather(from_x, "ey", axis=0, tiled=False)
    n_y = slot_rows.shape[0]
    flat_rows = slot_rows.reshape(-1, model_width)
    gate_act = jnp.dot(flat_rows, w_gate, preferred_element_type=jnp.float32)
    up_act = jnp.dot(flat_rows, w_up, preferred_element_type=jnp.float32)
    hidden = (jax.nn.silu(gate_act) * up_act).astype(jnp.bfloat16)
    hidden = hidden.reshape(n_y, n_x * MOST, hidden.shape[-1])
    hidden_here = lax.all_to_all(hidden, "ey", split_axis=0, concat_axis=0, tiled=True)
    me_y = lax.axis_index("ey")
    hidden_rel = jnp.take(hidden_here, (me_y + jnp.arange(n_y)) % n_y, axis=0)
    expert_out = None
    for d in range(n_y):
        part = jnp.dot(hidden_rel[d], down_all[d], preferred_element_type=jnp.float32)
        part = lax.reduce_precision(part, exponent_bits=8, mantissa_bits=7)
        expert_out = part if expert_out is None else expert_out + part
    expert_out = expert_out.reshape(n_x, block_rows, LANE)
    returned = lax.all_to_all(expert_out, "ex", split_axis=0, concat_axis=0, tiled=True)
    picked = returned.reshape(EXPERTS * MOST, model_width)[slot_ids]
    weights = route_weight.astype(jnp.float32) * FIXED_UNIT
    return jnp.sum(weights[:, :, None] * picked, axis=1)


def layer_terms(rows_in, gain_row, w_gate, w_up, down_all, expert_ids, route_weight):
    values = rows_in.astype(jnp.float32)
    inv_rms = lax.rsqrt(jnp.mean(values * values, axis=1, keepdims=True) + NORM_EPS)
    normed = (values * inv_rms * gain_row.astype(jnp.float32)).astype(jnp.bfloat16)
    branch = routed_branch(normed, expert_ids, route_weight, w_gate, w_up, down_all)
    return (values, branch)


def shards(acts, norm_gain, gate_w, up_w, down_w, route_ids, route_wts):
    section_index = lax.axis_index("pipe")
    rows_in = acts[0]
    gain_row = norm_gain[0]
    w_gate = gate_w[0, 0]
    w_up = up_w[0, 0]
    down_all = ring_gather(down_w[0, 0], "ey")
    values, branch = layer_terms(
        rows_in, gain_row, w_gate, w_up, down_all, route_ids[0, 0], route_wts[0, 0]
    )
    first_out = (values + branch).astype(jnp.bfloat16)
    arrived = shifted(first_out, "pipe", 1)
    values, branch = layer_terms(
        arrived, gain_row, w_gate, w_up, down_all, route_ids[0, 1], route_wts[0, 1]
    )
    second = (values + branch).astype(jnp.bfloat16)
    result_rows = jnp.where(section_index == 0, arrived, second)
    return result_rows[None]


def solution(mesh):
    n_x = EXPERTS
    n_pipe, n_expert = mesh.devices.shape
    split_mesh = Mesh(
        mesh.devices.reshape(n_pipe, n_x, n_expert // n_x), ("pipe", "ex", "ey")
    )
    rows = ("ex", "ey")
    return jax.shard_map(
        shards,
        mesh=split_mesh,
        in_specs=(
            P("pipe", rows, None),
            P("pipe", None),
            P("pipe", rows, None, None),
            P("pipe", rows, None, None),
            P("pipe", rows, None, None),
            P("pipe", None, rows, None),
            P("pipe", None, rows, None),
        ),
        out_specs=P("pipe", rows, None),
        check_vma=False,
    )
```

```python
import jax
import jax.numpy as jnp
from jax import lax
from jax.sharding import Mesh
from jax.sharding import PartitionSpec as P

EXPERTS = 4
MOST = 17
LANE = 128


NORM_EPS = 1e-06
FIXED_UNIT = 1.0 / 4096.0


def shifted(value, axis, steps):
    count = lax.axis_size(axis)
    pairs = [(source, (source + steps) % count) for source in range(count)]
    return lax.ppermute(value, axis, pairs)


def ring_gather(value, axis):
    count = lax.axis_size(axis)
    ahead, behind = {0: value}, {}
    forward, backward = value, value
    for step in range(1, count // 2 + 1):
        forward = shifted(forward, axis, 1)
        behind[step] = forward
        if step < count - step:
            backward = shifted(backward, axis, -1)
            ahead[step] = backward
    return [ahead[d] if d in ahead else behind[count - d] for d in range(count)]


def slot_index(expert_ids, capacity, experts):
    flat_ids = expert_ids.reshape(-1)
    onehot = (flat_ids[:, None] == jnp.arange(experts, dtype=jnp.int32)[None, :]).astype(jnp.int32)
    before = jnp.cumsum(onehot, axis=0) - onehot
    slot_rank = jnp.sum(before * onehot, axis=1)
    return (flat_ids * capacity + slot_rank).reshape(expert_ids.shape)


def place_rows(normed, slot_ids, slot_total):
    slot_marks = slot_ids[:, :, None] == jnp.arange(slot_total, dtype=jnp.int32)[None, None, :]
    placing = jnp.sum(slot_marks.astype(jnp.float32), axis=1).T.astype(jnp.bfloat16)
    return jnp.dot(placing, normed, preferred_element_type=jnp.float32).astype(jnp.bfloat16)


def slot_blocks(normed, slot_ids):
    model_width = normed.shape[1]
    placed = place_rows(normed, slot_ids, EXPERTS * MOST)
    return placed.reshape(EXPERTS, MOST * model_width // LANE, LANE)


def next_section_shift(value, steps):
    n_pipe = lax.axis_size("pipe")
    n_x = lax.axis_size("ex")
    pairs = []
    for p in range(n_pipe):
        for x in range(n_x):
            pairs.append((p * n_x + x, ((p + 1) % n_pipe) * n_x + (x + steps) % n_x))
    return lax.ppermute(value, ("pipe", "ex"), pairs)


def routed_branch(normed, expert_ids, route_weight, w_gate, w_up, down_all, from_x=None):
    n_x = lax.axis_size("ex")
    model_width = normed.shape[1]
    slot_ids = slot_index(expert_ids, MOST, EXPERTS)
    block_rows = MOST * model_width // LANE
    if from_x is None:
        per_expert = slot_blocks(normed, slot_ids)
        from_x = lax.all_to_all(per_expert, "ex", split_axis=0, concat_axis=0, tiled=True)
    slot_rows = lax.all_gather(from_x, "ey", axis=0, tiled=False)
    n_y = slot_rows.shape[0]
    flat_rows = slot_rows.reshape(-1, model_width)
    gate_act = jnp.dot(flat_rows, w_gate, preferred_element_type=jnp.float32)
    up_act = jnp.dot(flat_rows, w_up, preferred_element_type=jnp.float32)
    hidden = (jax.nn.silu(gate_act) * up_act).astype(jnp.bfloat16)
    hidden = hidden.reshape(n_y, n_x * MOST, hidden.shape[-1])
    hidden_here = lax.all_to_all(hidden, "ey", split_axis=0, concat_axis=0, tiled=True)
    me_y = lax.axis_index("ey")
    hidden_rel = jnp.take(hidden_here, (me_y + jnp.arange(n_y)) % n_y, axis=0)
    expert_out = None
    for d in range(n_y):
        part = jnp.dot(hidden_rel[d], down_all[d], preferred_element_type=jnp.float32)
        part = lax.reduce_precision(part, exponent_bits=8, mantissa_bits=7)
        expert_out = part if expert_out is None else expert_out + part
    expert_out = expert_out.reshape(n_x, block_rows, LANE)
    returned = lax.all_to_all(expert_out, "ex", split_axis=0, concat_axis=0, tiled=True)
    picked = returned.reshape(EXPERTS * MOST, model_width)[slot_ids]
    weights = route_weight.astype(jnp.float32) * FIXED_UNIT
    return jnp.sum(weights[:, :, None] * picked, axis=1)


def normalize(rows_in, gain_row):
    values = rows_in.astype(jnp.float32)
    inv_rms = lax.rsqrt(jnp.mean(values * values, axis=1, keepdims=True) + NORM_EPS)
    normed = (values * inv_rms * gain_row.astype(jnp.float32)).astype(jnp.bfloat16)
    return values, normed


def layer_terms(rows_in, gain_row, w_gate, w_up, down_all, expert_ids, route_weight, from_x=None):
    values, normed = normalize(rows_in, gain_row)
    branch = routed_branch(normed, expert_ids, route_weight, w_gate, w_up, down_all, from_x)
    return (values, branch)


def shards(acts, norm_gain, gate_w, up_w, down_w, route_ids, route_wts):
    section_index = lax.axis_index("pipe")
    rows_in = acts[0]
    gain_row = norm_gain[0]
    w_gate = gate_w[0, 0]
    w_up = up_w[0, 0]
    down_all = ring_gather(down_w[0, 0], "ey")
    gain_next = shifted(gain_row, "pipe", -1)
    ids_next = shifted(route_ids[0, 1], "pipe", -1)
    values, branch = layer_terms(
        rows_in, gain_row, w_gate, w_up, down_all, route_ids[0, 0], route_wts[0, 0]
    )
    first_out = (values + branch).astype(jnp.bfloat16)
    arrived = shifted(first_out, "pipe", 1)
    me_x = lax.axis_index("ex")
    _, normed_next = normalize(first_out, gain_next)
    blocks_next = slot_blocks(normed_next, slot_index(ids_next, MOST, EXPERTS))
    received = []
    for d in range(EXPERTS):
        block = lax.dynamic_index_in_dim(blocks_next, (me_x + d) % EXPERTS, 0, keepdims=False)
        received.append(next_section_shift(block, d))
    received = jnp.stack(received, axis=0)
    from_x = jnp.take(received, (me_x - jnp.arange(EXPERTS)) % EXPERTS, axis=0)
    values, branch = layer_terms(
        arrived, gain_row, w_gate, w_up, down_all, route_ids[0, 1], route_wts[0, 1], from_x
    )
    second = (values + branch).astype(jnp.bfloat16)
    result_rows = jnp.where(section_index == 0, arrived, second)
    return result_rows[None]


def solution(mesh):
    n_x = EXPERTS
    n_pipe, n_expert = mesh.devices.shape
    split_mesh = Mesh(
        mesh.devices.reshape(n_pipe, n_x, n_expert // n_x), ("pipe", "ex", "ey")
    )
    rows = ("ex", "ey")
    return jax.shard_map(
        shards,
        mesh=split_mesh,
        in_specs=(
            P("pipe", rows, None),
            P("pipe", None),
            P("pipe", rows, None, None),
            P("pipe", rows, None, None),
            P("pipe", rows, None, None),
            P("pipe", None, rows, None),
            P("pipe", None, rows, None),
        ),
        out_specs=P("pipe", rows, None),
        check_vma=False,
    )
```

```python
import jax
import jax.numpy as jnp
from jax import lax
from jax.sharding import Mesh
from jax.sharding import PartitionSpec as P

EXPERTS = 4
MOST = 17
LANE = 128


NORM_EPS = 1e-06
FIXED_UNIT = 1.0 / 4096.0


def shifted(value, axis, steps):
    count = lax.axis_size(axis)
    pairs = [(source, (source + steps) % count) for source in range(count)]
    return lax.ppermute(value, axis, pairs)


def ring_gather(value, axis):
    count = lax.axis_size(axis)
    ahead, behind = {0: value}, {}
    forward, backward = value, value
    for step in range(1, count // 2 + 1):
        forward = shifted(forward, axis, 1)
        behind[step] = forward
        if step < count - step:
            backward = shifted(backward, axis, -1)
            ahead[step] = backward
    return [ahead[d] if d in ahead else behind[count - d] for d in range(count)]


def slot_index(expert_ids, capacity, experts):
    flat_ids = expert_ids.reshape(-1)
    onehot = (flat_ids[:, None] == jnp.arange(experts, dtype=jnp.int32)[None, :]).astype(jnp.int32)
    before = jnp.cumsum(onehot, axis=0) - onehot
    slot_rank = jnp.sum(before * onehot, axis=1)
    return (flat_ids * capacity + slot_rank).reshape(expert_ids.shape)


def place_rows(normed, slot_ids, slot_total):
    slot_marks = slot_ids[:, :, None] == jnp.arange(slot_total, dtype=jnp.int32)[None, None, :]
    placing = jnp.sum(slot_marks.astype(jnp.float32), axis=1).T.astype(jnp.bfloat16)
    return jnp.dot(placing, normed, preferred_element_type=jnp.float32).astype(jnp.bfloat16)


def routed_branch(normed, expert_ids, route_weight, w_gate, w_up, down_all):
    n_x = lax.axis_size("ex")
    model_width = normed.shape[1]
    slot_ids = slot_index(expert_ids, MOST, EXPERTS)
    block_rows = MOST * model_width // LANE
    per_expert = place_rows(normed, slot_ids, EXPERTS * MOST).reshape(EXPERTS, block_rows, LANE)
    from_x = lax.all_to_all(per_expert, "ex", split_axis=0, concat_axis=0, tiled=True)
    slot_rows = lax.all_gather(from_x, "ey", axis=0, tiled=False)
    n_y = slot_rows.shape[0]
    flat_rows = slot_rows.reshape(-1, model_width)
    gate_act = jnp.dot(flat_rows, w_gate, preferred_element_type=jnp.float32)
    up_act = jnp.dot(flat_rows, w_up, preferred_element_type=jnp.float32)
    hidden = (jax.nn.silu(gate_act) * up_act).astype(jnp.bfloat16)
    hidden = hidden.reshape(n_y, n_x * MOST, hidden.shape[-1])
    hidden_here = lax.all_to_all(hidden, "ey", split_axis=0, concat_axis=0, tiled=True)
    me_y = lax.axis_index("ey")
    hidden_rel = jnp.take(hidden_here, (me_y + jnp.arange(n_y)) % n_y, axis=0)
    if isinstance(down_all, list):
        expert_out = None
        for d in range(n_y):
            part = jnp.dot(hidden_rel[d], down_all[d], preferred_element_type=jnp.float32)
            part = lax.reduce_precision(part, exponent_bits=8, mantissa_bits=7)
            expert_out = part if expert_out is None else expert_out + part
    else:
        parts = jnp.einsum("jrh,jhd->jrd", hidden_rel, down_all, preferred_element_type=jnp.float32)
        parts = lax.reduce_precision(parts, exponent_bits=8, mantissa_bits=7)
        expert_out = jnp.sum(parts, axis=0)
    expert_out = expert_out.reshape(n_x, block_rows, LANE)
    returned = lax.all_to_all(expert_out, "ex", split_axis=0, concat_axis=0, tiled=True)
    picked = returned.reshape(EXPERTS * MOST, model_width)[slot_ids]
    weights = route_weight.astype(jnp.float32) * FIXED_UNIT
    return jnp.sum(weights[:, :, None] * picked, axis=1)


def layer_terms(rows_in, gain_row, w_gate, w_up, down_all, expert_ids, route_weight):
    values = rows_in.astype(jnp.float32)
    inv_rms = lax.rsqrt(jnp.mean(values * values, axis=1, keepdims=True) + NORM_EPS)
    normed = (values * inv_rms * gain_row.astype(jnp.float32)).astype(jnp.bfloat16)
    branch = routed_branch(normed, expert_ids, route_weight, w_gate, w_up, down_all)
    return (values, branch)


def shards(acts, norm_gain, gate_w, up_w, down_w, route_ids, route_wts):
    section_index = lax.axis_index("pipe")
    rows_in = acts[0]
    gain_row = norm_gain[0]
    w_gate = gate_w[0, 0]
    w_up = up_w[0, 0]
    down_all = ring_gather(down_w[0, 0], "ey")
    values, branch = layer_terms(
        rows_in, gain_row, w_gate, w_up, down_all, route_ids[0, 0], route_wts[0, 0]
    )
    first_out = (values + branch).astype(jnp.bfloat16)
    arrived = shifted(first_out, "pipe", 1)
    first_out, down_all = lax.optimization_barrier((first_out, down_all))
    down_stack = jnp.stack(down_all, axis=0)
    values, branch = layer_terms(
        arrived, gain_row, w_gate, w_up, down_stack, route_ids[0, 1], route_wts[0, 1]
    )
    second = (values + branch).astype(jnp.bfloat16)
    result_rows = jnp.where(section_index == 0, arrived, second)
    return result_rows[None]


def solution(mesh):
    n_x = EXPERTS
    n_pipe, n_expert = mesh.devices.shape
    split_mesh = Mesh(
        mesh.devices.reshape(n_pipe, n_x, n_expert // n_x), ("pipe", "ex", "ey")
    )
    rows = ("ex", "ey")
    return jax.shard_map(
        shards,
        mesh=split_mesh,
        in_specs=(
            P("pipe", rows, None),
            P("pipe", None),
            P("pipe", rows, None, None),
            P("pipe", rows, None, None),
            P("pipe", rows, None, None),
            P("pipe", None, rows, None),
            P("pipe", None, rows, None),
        ),
        out_specs=P("pipe", rows, None),
        check_vma=False,
    )
```

```python
import jax
import jax.numpy as jnp
from jax import lax
from jax.sharding import Mesh
from jax.sharding import PartitionSpec as P

EXPERTS = 4
MOST = 17
LANE = 128


NORM_EPS = 1e-06
FIXED_UNIT = 1.0 / 4096.0


def shifted(value, axis, steps):
    count = lax.axis_size(axis)
    pairs = [(source, (source + steps) % count) for source in range(count)]
    return lax.ppermute(value, axis, pairs)


def ring_gather(value, axis):
    count = lax.axis_size(axis)
    ahead, behind = {0: value}, {}
    forward, backward = value, value
    for step in range(1, count // 2 + 1):
        forward = shifted(forward, axis, 1)
        behind[step] = forward
        if step < count - step:
            backward = shifted(backward, axis, -1)
            ahead[step] = backward
    return [ahead[d] if d in ahead else behind[count - d] for d in range(count)]


def slot_index(expert_ids, capacity, experts):
    flat_ids = expert_ids.reshape(-1)
    onehot = (flat_ids[:, None] == jnp.arange(experts, dtype=jnp.int32)[None, :]).astype(jnp.int32)
    before = jnp.cumsum(onehot, axis=0) - onehot
    slot_rank = jnp.sum(before * onehot, axis=1)
    return (flat_ids * capacity + slot_rank).reshape(expert_ids.shape)


def place_rows(normed, slot_ids, slot_total):
    slot_marks = slot_ids[:, :, None] == jnp.arange(slot_total, dtype=jnp.int32)[None, None, :]
    placing = jnp.sum(slot_marks.astype(jnp.float32), axis=1).T.astype(jnp.bfloat16)
    return jnp.dot(placing, normed, preferred_element_type=jnp.float32).astype(jnp.bfloat16)


def routed_branch(normed, expert_ids, route_weight, w_gate, w_up, down_all):
    n_x = lax.axis_size("ex")
    model_width = normed.shape[1]
    slot_ids = slot_index(expert_ids, MOST, EXPERTS)
    block_rows = MOST * model_width // LANE
    per_expert = place_rows(normed, slot_ids, EXPERTS * MOST).reshape(EXPERTS, block_rows, LANE)
    from_x = lax.all_to_all(per_expert, "ex", split_axis=0, concat_axis=0, tiled=True)
    me_y = lax.axis_index("ey")
    if isinstance(down_all, list):
        slot_rows = lax.all_gather(from_x, "ey", axis=0, tiled=False)
        n_y = slot_rows.shape[0]
        flat_rows = slot_rows.reshape(-1, model_width)
        gate_act = jnp.dot(flat_rows, w_gate, preferred_element_type=jnp.float32)
        up_act = jnp.dot(flat_rows, w_up, preferred_element_type=jnp.float32)
        hidden = (jax.nn.silu(gate_act) * up_act).astype(jnp.bfloat16)
        hidden = hidden.reshape(n_y, n_x * MOST, hidden.shape[-1])
    else:
        blocks = ring_gather(from_x, "ey")
        n_y = len(blocks)
        served = []
        for block in blocks:
            rows = block.reshape(-1, model_width)
            gate_act = jnp.dot(rows, w_gate, preferred_element_type=jnp.float32)
            up_act = jnp.dot(rows, w_up, preferred_element_type=jnp.float32)
            served.append((jax.nn.silu(gate_act) * up_act).astype(jnp.bfloat16))
        hidden = jnp.take(jnp.stack(served, axis=0), (jnp.arange(n_y) - me_y) % n_y, axis=0)
    hidden_here = lax.all_to_all(hidden, "ey", split_axis=0, concat_axis=0, tiled=True)
    hidden_rel = jnp.take(hidden_here, (me_y + jnp.arange(n_y)) % n_y, axis=0)
    if isinstance(down_all, list):
        expert_out = None
        for d in range(n_y):
            part = jnp.dot(hidden_rel[d], down_all[d], preferred_element_type=jnp.float32)
            part = lax.reduce_precision(part, exponent_bits=8, mantissa_bits=7)
            expert_out = part if expert_out is None else expert_out + part
    else:
        parts = jnp.einsum("jrh,jhd->jrd", hidden_rel, down_all, preferred_element_type=jnp.float32)
        parts = lax.reduce_precision(parts, exponent_bits=8, mantissa_bits=7)
        expert_out = jnp.sum(parts, axis=0)
    expert_out = expert_out.reshape(n_x, block_rows, LANE)
    returned = lax.all_to_all(expert_out, "ex", split_axis=0, concat_axis=0, tiled=True)
    picked = returned.reshape(EXPERTS * MOST, model_width)[slot_ids]
    weights = route_weight.astype(jnp.float32) * FIXED_UNIT
    return jnp.sum(weights[:, :, None] * picked, axis=1)


def layer_terms(rows_in, gain_row, w_gate, w_up, down_all, expert_ids, route_weight):
    values = rows_in.astype(jnp.float32)
    inv_rms = lax.rsqrt(jnp.mean(values * values, axis=1, keepdims=True) + NORM_EPS)
    normed = (values * inv_rms * gain_row.astype(jnp.float32)).astype(jnp.bfloat16)
    branch = routed_branch(normed, expert_ids, route_weight, w_gate, w_up, down_all)
    return (values, branch)


def shards(acts, norm_gain, gate_w, up_w, down_w, route_ids, route_wts):
    section_index = lax.axis_index("pipe")
    rows_in = acts[0]
    gain_row = norm_gain[0]
    w_gate = gate_w[0, 0]
    w_up = up_w[0, 0]
    down_all = ring_gather(down_w[0, 0], "ey")
    values, branch = layer_terms(
        rows_in, gain_row, w_gate, w_up, down_all, route_ids[0, 0], route_wts[0, 0]
    )
    first_out = (values + branch).astype(jnp.bfloat16)
    arrived = shifted(first_out, "pipe", 1)
    first_out, down_all = lax.optimization_barrier((first_out, down_all))
    down_stack = jnp.stack(down_all, axis=0)
    values, branch = layer_terms(
        arrived, gain_row, w_gate, w_up, down_stack, route_ids[0, 1], route_wts[0, 1]
    )
    second = (values + branch).astype(jnp.bfloat16)
    result_rows = jnp.where(section_index == 0, arrived, second)
    return result_rows[None]


def solution(mesh):
    n_x = EXPERTS
    n_pipe, n_expert = mesh.devices.shape
    split_mesh = Mesh(
        mesh.devices.reshape(n_pipe, n_x, n_expert // n_x), ("pipe", "ex", "ey")
    )
    rows = ("ex", "ey")
    return jax.shard_map(
        shards,
        mesh=split_mesh,
        in_specs=(
            P("pipe", rows, None),
            P("pipe", None),
            P("pipe", rows, None, None),
            P("pipe", rows, None, None),
            P("pipe", rows, None, None),
            P("pipe", None, rows, None),
            P("pipe", None, rows, None),
        ),
        out_specs=P("pipe", rows, None),
        check_vma=False,
    )
```

```python
import jax
import jax.numpy as jnp
from jax import lax
from jax.sharding import Mesh
from jax.sharding import PartitionSpec as P

EXPERTS = 4
MOST = 17
LANE = 128
SUBLANE = 8


NORM_EPS = 1e-06
FIXED_UNIT = 1.0 / 4096.0


def shifted(value, axis, steps):
    count = lax.axis_size(axis)
    pairs = [(source, (source + steps) % count) for source in range(count)]
    return lax.ppermute(value, axis, pairs)


def ring_gather(value, axis):
    count = lax.axis_size(axis)
    ahead, behind = {0: value}, {}
    forward, backward = value, value
    for step in range(1, count // 2 + 1):
        forward = shifted(forward, axis, 1)
        behind[step] = forward
        if step < count - step:
            backward = shifted(backward, axis, -1)
            ahead[step] = backward
    return [ahead[d] if d in ahead else behind[count - d] for d in range(count)]


def slot_index(expert_ids, capacity, experts):
    flat_ids = expert_ids.reshape(-1)
    onehot = (flat_ids[:, None] == jnp.arange(experts, dtype=jnp.int32)[None, :]).astype(jnp.int32)
    before = jnp.cumsum(onehot, axis=0) - onehot
    slot_rank = jnp.sum(before * onehot, axis=1)
    return (flat_ids * capacity + slot_rank).reshape(expert_ids.shape)


def place_rows(normed, slot_ids, slot_total):
    slot_marks = slot_ids[:, :, None] == jnp.arange(slot_total, dtype=jnp.int32)[None, None, :]
    placing = jnp.sum(slot_marks.astype(jnp.float32), axis=1).T.astype(jnp.bfloat16)
    return jnp.dot(placing, normed, preferred_element_type=jnp.float32).astype(jnp.bfloat16)


def routed_branch(normed, expert_ids, route_weight, w_gate, w_up, down_all):
    n_x = lax.axis_size("ex")
    model_width = normed.shape[1]
    slot_ids = slot_index(expert_ids, MOST, EXPERTS)
    block_rows = MOST * model_width // LANE
    per_expert = place_rows(normed, slot_ids, EXPERTS * MOST).reshape(EXPERTS, block_rows, LANE)
    from_x = lax.all_to_all(per_expert, "ex", split_axis=0, concat_axis=0, tiled=True)
    if isinstance(down_all, list):
        slot_rows = lax.all_gather(from_x, "ey", axis=0, tiled=False)
        n_y = slot_rows.shape[0]
        flat_rows = slot_rows.reshape(-1, model_width)
    else:
        held = n_x * MOST
        padded = -(-held // SUBLANE) * SUBLANE
        own_rows = jnp.pad(from_x.reshape(held, model_width), ((0, padded - held), (0, 0)))
        slot_rows = lax.all_gather(own_rows, "ey", axis=0, tiled=False)
        n_y = slot_rows.shape[0]
        flat_rows = slot_rows.reshape(-1, model_width)
    gate_act = jnp.dot(flat_rows, w_gate, preferred_element_type=jnp.float32)
    up_act = jnp.dot(flat_rows, w_up, preferred_element_type=jnp.float32)
    hidden = (jax.nn.silu(gate_act) * up_act).astype(jnp.bfloat16)
    hidden = hidden.reshape(n_y, -1, hidden.shape[-1])[:, : n_x * MOST]
    hidden_here = lax.all_to_all(hidden, "ey", split_axis=0, concat_axis=0, tiled=True)
    me_y = lax.axis_index("ey")
    hidden_rel = jnp.take(hidden_here, (me_y + jnp.arange(n_y)) % n_y, axis=0)
    if isinstance(down_all, list):
        expert_out = None
        for d in range(n_y):
            part = jnp.dot(hidden_rel[d], down_all[d], preferred_element_type=jnp.float32)
            part = lax.reduce_precision(part, exponent_bits=8, mantissa_bits=7)
            expert_out = part if expert_out is None else expert_out + part
    else:
        parts = jnp.einsum("jrh,jhd->jrd", hidden_rel, down_all, preferred_element_type=jnp.float32)
        parts = lax.reduce_precision(parts, exponent_bits=8, mantissa_bits=7)
        expert_out = jnp.sum(parts, axis=0)
    expert_out = expert_out.reshape(n_x, block_rows, LANE)
    returned = lax.all_to_all(expert_out, "ex", split_axis=0, concat_axis=0, tiled=True)
    picked = returned.reshape(EXPERTS * MOST, model_width)[slot_ids]
    weights = route_weight.astype(jnp.float32) * FIXED_UNIT
    return jnp.sum(weights[:, :, None] * picked, axis=1)


def layer_terms(rows_in, gain_row, w_gate, w_up, down_all, expert_ids, route_weight):
    values = rows_in.astype(jnp.float32)
    inv_rms = lax.rsqrt(jnp.mean(values * values, axis=1, keepdims=True) + NORM_EPS)
    normed = (values * inv_rms * gain_row.astype(jnp.float32)).astype(jnp.bfloat16)
    branch = routed_branch(normed, expert_ids, route_weight, w_gate, w_up, down_all)
    return (values, branch)


def shards(acts, norm_gain, gate_w, up_w, down_w, route_ids, route_wts):
    section_index = lax.axis_index("pipe")
    rows_in = acts[0]
    gain_row = norm_gain[0]
    w_gate = gate_w[0, 0]
    w_up = up_w[0, 0]
    down_all = ring_gather(down_w[0, 0], "ey")
    values, branch = layer_terms(
        rows_in, gain_row, w_gate, w_up, down_all, route_ids[0, 0], route_wts[0, 0]
    )
    first_out = (values + branch).astype(jnp.bfloat16)
    arrived = shifted(first_out, "pipe", 1)
    first_out, down_all = lax.optimization_barrier((first_out, down_all))
    down_stack = jnp.stack(down_all, axis=0)
    values, branch = layer_terms(
        arrived, gain_row, w_gate, w_up, down_stack, route_ids[0, 1], route_wts[0, 1]
    )
    second = (values + branch).astype(jnp.bfloat16)
    result_rows = jnp.where(section_index == 0, arrived, second)
    return result_rows[None]


def solution(mesh):
    n_x = EXPERTS
    n_pipe, n_expert = mesh.devices.shape
    split_mesh = Mesh(
        mesh.devices.reshape(n_pipe, n_x, n_expert // n_x), ("pipe", "ex", "ey")
    )
    rows = ("ex", "ey")
    return jax.shard_map(
        shards,
        mesh=split_mesh,
        in_specs=(
            P("pipe", rows, None),
            P("pipe", None),
            P("pipe", rows, None, None),
            P("pipe", rows, None, None),
            P("pipe", rows, None, None),
            P("pipe", None, rows, None),
            P("pipe", None, rows, None),
        ),
        out_specs=P("pipe", rows, None),
        check_vma=False,
    )
```

```python
import jax
import jax.numpy as jnp
from jax import lax
from jax.sharding import Mesh
from jax.sharding import PartitionSpec as P

EXPERTS = 4
MOST = 17
LANE = 128
SUBLANE = 8


NORM_EPS = 1e-06
FIXED_UNIT = 1.0 / 4096.0


def shifted(value, axis, steps):
    count = lax.axis_size(axis)
    pairs = [(source, (source + steps) % count) for source in range(count)]
    return lax.ppermute(value, axis, pairs)


def ring_gather(value, axis):
    count = lax.axis_size(axis)
    ahead, behind = {0: value}, {}
    forward, backward = value, value
    for step in range(1, count // 2 + 1):
        forward = shifted(forward, axis, 1)
        behind[step] = forward
        if step < count - step:
            backward = shifted(backward, axis, -1)
            ahead[step] = backward
    return [ahead[d] if d in ahead else behind[count - d] for d in range(count)]


def slot_index(expert_ids, capacity, experts):
    flat_ids = expert_ids.reshape(-1)
    onehot = (flat_ids[:, None] == jnp.arange(experts, dtype=jnp.int32)[None, :]).astype(jnp.int32)
    before = jnp.cumsum(onehot, axis=0) - onehot
    slot_rank = jnp.sum(before * onehot, axis=1)
    return (flat_ids * capacity + slot_rank).reshape(expert_ids.shape)


def place_rows(normed, slot_ids, slot_total):
    slot_marks = slot_ids[:, :, None] == jnp.arange(slot_total, dtype=jnp.int32)[None, None, :]
    placing = jnp.sum(slot_marks.astype(jnp.float32), axis=1).T.astype(jnp.bfloat16)
    return jnp.dot(placing, normed, preferred_element_type=jnp.float32).astype(jnp.bfloat16)


def routed_branch(normed, expert_ids, route_weight, w_gate, w_up, down_all):
    n_x = lax.axis_size("ex")
    model_width = normed.shape[1]
    slot_ids = slot_index(expert_ids, MOST, EXPERTS)
    block_rows = MOST * model_width // LANE
    per_expert = place_rows(normed, slot_ids, EXPERTS * MOST).reshape(EXPERTS, block_rows, LANE)
    from_x = lax.all_to_all(per_expert, "ex", split_axis=0, concat_axis=0, tiled=True)
    held = n_x * MOST
    padded = -(-held // SUBLANE) * SUBLANE
    own_rows = jnp.pad(from_x.reshape(held, model_width), ((0, padded - held), (0, 0)))
    slot_rows = lax.all_gather(own_rows, "ey", axis=0, tiled=False)
    n_y = slot_rows.shape[0]
    flat_rows = slot_rows.reshape(-1, model_width)
    gate_act = jnp.dot(flat_rows, w_gate, preferred_element_type=jnp.float32)
    up_act = jnp.dot(flat_rows, w_up, preferred_element_type=jnp.float32)
    hidden = (jax.nn.silu(gate_act) * up_act).astype(jnp.bfloat16)
    hidden = hidden.reshape(n_y, -1, hidden.shape[-1])[:, : n_x * MOST]
    hidden_here = lax.all_to_all(hidden, "ey", split_axis=0, concat_axis=0, tiled=True)
    me_y = lax.axis_index("ey")
    hidden_rel = jnp.take(hidden_here, (me_y + jnp.arange(n_y)) % n_y, axis=0)
    if isinstance(down_all, list):
        expert_out = None
        for d in range(n_y):
            part = jnp.dot(hidden_rel[d], down_all[d], preferred_element_type=jnp.float32)
            part = lax.reduce_precision(part, exponent_bits=8, mantissa_bits=7)
            expert_out = part if expert_out is None else expert_out + part
    else:
        parts = jnp.einsum("jrh,jhd->jrd", hidden_rel, down_all, preferred_element_type=jnp.float32)
        parts = lax.reduce_precision(parts, exponent_bits=8, mantissa_bits=7)
        expert_out = jnp.sum(parts, axis=0)
    expert_out = expert_out.reshape(n_x, block_rows, LANE)
    returned = lax.all_to_all(expert_out, "ex", split_axis=0, concat_axis=0, tiled=True)
    picked = returned.reshape(EXPERTS * MOST, model_width)[slot_ids]
    weights = route_weight.astype(jnp.float32) * FIXED_UNIT
    return jnp.sum(weights[:, :, None] * picked, axis=1)


def layer_terms(rows_in, gain_row, w_gate, w_up, down_all, expert_ids, route_weight):
    values = rows_in.astype(jnp.float32)
    inv_rms = lax.rsqrt(jnp.mean(values * values, axis=1, keepdims=True) + NORM_EPS)
    normed = (values * inv_rms * gain_row.astype(jnp.float32)).astype(jnp.bfloat16)
    branch = routed_branch(normed, expert_ids, route_weight, w_gate, w_up, down_all)
    return (values, branch)


def shards(acts, norm_gain, gate_w, up_w, down_w, route_ids, route_wts):
    section_index = lax.axis_index("pipe")
    rows_in = acts[0]
    gain_row = norm_gain[0]
    w_gate = gate_w[0, 0]
    w_up = up_w[0, 0]
    down_all = ring_gather(down_w[0, 0], "ey")
    values, branch = layer_terms(
        rows_in, gain_row, w_gate, w_up, down_all, route_ids[0, 0], route_wts[0, 0]
    )
    first_out = (values + branch).astype(jnp.bfloat16)
    arrived = shifted(first_out, "pipe", 1)
    first_out, down_all = lax.optimization_barrier((first_out, down_all))
    down_stack = jnp.stack(down_all, axis=0)
    values, branch = layer_terms(
        arrived, gain_row, w_gate, w_up, down_stack, route_ids[0, 1], route_wts[0, 1]
    )
    second = (values + branch).astype(jnp.bfloat16)
    result_rows = jnp.where(section_index == 0, arrived, second)
    return result_rows[None]


def solution(mesh):
    n_x = EXPERTS
    n_pipe, n_expert = mesh.devices.shape
    split_mesh = Mesh(
        mesh.devices.reshape(n_pipe, n_x, n_expert // n_x), ("pipe", "ex", "ey")
    )
    rows = ("ex", "ey")
    return jax.shard_map(
        shards,
        mesh=split_mesh,
        in_specs=(
            P("pipe", rows, None),
            P("pipe", None),
            P("pipe", rows, None, None),
            P("pipe", rows, None, None),
            P("pipe", rows, None, None),
            P("pipe", None, rows, None),
            P("pipe", None, rows, None),
        ),
        out_specs=P("pipe", rows, None),
        check_vma=False,
    )
```

```python
import jax
import jax.numpy as jnp
from jax import lax
from jax.sharding import Mesh
from jax.sharding import PartitionSpec as P

EXPERTS = 4
MOST = 17
LANE = 128
SUBLANE = 8


NORM_EPS = 1e-06
FIXED_UNIT = 1.0 / 4096.0


def shifted(value, axis, steps):
    count = lax.axis_size(axis)
    pairs = [(source, (source + steps) % count) for source in range(count)]
    return lax.ppermute(value, axis, pairs)


def ring_gather(value, axis):
    count = lax.axis_size(axis)
    ahead, behind = {0: value}, {}
    forward, backward = value, value
    for step in range(1, count // 2 + 1):
        forward = shifted(forward, axis, 1)
        behind[step] = forward
        if step < count - step:
            backward = shifted(backward, axis, -1)
            ahead[step] = backward
    return [ahead[d] if d in ahead else behind[count - d] for d in range(count)]


def slot_index(expert_ids, capacity, experts):
    flat_ids = expert_ids.reshape(-1)
    onehot = (flat_ids[:, None] == jnp.arange(experts, dtype=jnp.int32)[None, :]).astype(jnp.int32)
    before = jnp.cumsum(onehot, axis=0) - onehot
    slot_rank = jnp.sum(before * onehot, axis=1)
    return (flat_ids * capacity + slot_rank).reshape(expert_ids.shape)


def place_rows(normed, slot_ids, slot_total):
    slot_marks = slot_ids[:, :, None] == jnp.arange(slot_total, dtype=jnp.int32)[None, None, :]
    placing = jnp.sum(slot_marks.astype(jnp.float32), axis=1).T.astype(jnp.bfloat16)
    return jnp.dot(placing, normed, preferred_element_type=jnp.float32).astype(jnp.bfloat16)


def routed_branch(normed, expert_ids, route_weight, w_gate, w_up, down_all):
    n_x = lax.axis_size("ex")
    model_width = normed.shape[1]
    slot_ids = slot_index(expert_ids, MOST, EXPERTS)
    block_rows = MOST * model_width // LANE
    per_expert = place_rows(normed, slot_ids, EXPERTS * MOST).reshape(EXPERTS, block_rows, LANE)
    from_x = lax.all_to_all(per_expert, "ex", split_axis=0, concat_axis=0, tiled=True)
    held = n_x * MOST
    padded = -(-held // SUBLANE) * SUBLANE
    own_rows = jnp.pad(from_x.reshape(held, model_width), ((0, padded - held), (0, 0)))
    slot_rows = lax.all_gather(own_rows, "ey", axis=0, tiled=False)
    if callable(down_all):
        slot_rows, down_all = down_all(slot_rows)
    n_y = slot_rows.shape[0]
    flat_rows = slot_rows.reshape(-1, model_width)
    gate_act = jnp.dot(flat_rows, w_gate, preferred_element_type=jnp.float32)
    up_act = jnp.dot(flat_rows, w_up, preferred_element_type=jnp.float32)
    hidden = (jax.nn.silu(gate_act) * up_act).astype(jnp.bfloat16)
    hidden = hidden.reshape(n_y, -1, hidden.shape[-1])[:, : n_x * MOST]
    hidden_here = lax.all_to_all(hidden, "ey", split_axis=0, concat_axis=0, tiled=True)
    me_y = lax.axis_index("ey")
    hidden_rel = jnp.take(hidden_here, (me_y + jnp.arange(n_y)) % n_y, axis=0)
    if isinstance(down_all, list):
        expert_out = None
        for d in range(n_y):
            part = jnp.dot(hidden_rel[d], down_all[d], preferred_element_type=jnp.float32)
            part = lax.reduce_precision(part, exponent_bits=8, mantissa_bits=7)
            expert_out = part if expert_out is None else expert_out + part
    else:
        parts = jnp.einsum("jrh,jhd->jrd", hidden_rel, down_all, preferred_element_type=jnp.float32)
        parts = lax.reduce_precision(parts, exponent_bits=8, mantissa_bits=7)
        expert_out = jnp.sum(parts, axis=0)
    expert_out = expert_out.reshape(n_x, block_rows, LANE)
    returned = lax.all_to_all(expert_out, "ex", split_axis=0, concat_axis=0, tiled=True)
    picked = returned.reshape(EXPERTS * MOST, model_width)[slot_ids]
    weights = route_weight.astype(jnp.float32) * FIXED_UNIT
    return jnp.sum(weights[:, :, None] * picked, axis=1)


def layer_terms(rows_in, gain_row, w_gate, w_up, down_all, expert_ids, route_weight):
    values = rows_in.astype(jnp.float32)
    inv_rms = lax.rsqrt(jnp.mean(values * values, axis=1, keepdims=True) + NORM_EPS)
    normed = (values * inv_rms * gain_row.astype(jnp.float32)).astype(jnp.bfloat16)
    branch = routed_branch(normed, expert_ids, route_weight, w_gate, w_up, down_all)
    return (values, branch)


def shards(acts, norm_gain, gate_w, up_w, down_w, route_ids, route_wts):
    section_index = lax.axis_index("pipe")
    rows_in = acts[0]
    gain_row = norm_gain[0]
    w_gate = gate_w[0, 0]
    w_up = up_w[0, 0]
    own_down = down_w[0, 0]
    forward_1 = shifted(own_down, "ey", 1)
    backward_1 = shifted(own_down, "ey", -1)
    forward_2 = shifted(forward_1, "ey", 1)
    backward_2 = shifted(backward_1, "ey", -1)
    gathered = []

    def ring_rest(slot_rows):
        slot_rows, forward, backward = lax.optimization_barrier((slot_rows, forward_2, backward_2))
        forward_3 = shifted(forward, "ey", 1)
        backward_3 = shifted(backward, "ey", -1)
        forward_4 = shifted(forward_3, "ey", 1)
        gathered.append([own_down, backward_1, backward, backward_3, forward_4, forward_3, forward, forward_1])
        return slot_rows, gathered[0]

    values, branch = layer_terms(
        rows_in, gain_row, w_gate, w_up, ring_rest, route_ids[0, 0], route_wts[0, 0]
    )
    down_all = gathered[0]
    first_out = (values + branch).astype(jnp.bfloat16)
    arrived = shifted(first_out, "pipe", 1)
    first_out, down_all = lax.optimization_barrier((first_out, down_all))
    down_stack = jnp.stack(down_all, axis=0)
    values, branch = layer_terms(
        arrived, gain_row, w_gate, w_up, down_stack, route_ids[0, 1], route_wts[0, 1]
    )
    second = (values + branch).astype(jnp.bfloat16)
    result_rows = jnp.where(section_index == 0, arrived, second)
    return result_rows[None]


def solution(mesh):
    n_x = EXPERTS
    n_pipe, n_expert = mesh.devices.shape
    split_mesh = Mesh(
        mesh.devices.reshape(n_pipe, n_x, n_expert // n_x), ("pipe", "ex", "ey")
    )
    rows = ("ex", "ey")
    return jax.shard_map(
        shards,
        mesh=split_mesh,
        in_specs=(
            P("pipe", rows, None),
            P("pipe", None),
            P("pipe", rows, None, None),
            P("pipe", rows, None, None),
            P("pipe", rows, None, None),
            P("pipe", None, rows, None),
            P("pipe", None, rows, None),
        ),
        out_specs=P("pipe", rows, None),
        check_vma=False,
    )
```

```python
import jax
import jax.numpy as jnp
from jax import lax
from jax.sharding import Mesh
from jax.sharding import PartitionSpec as P

EXPERTS = 4
MOST = 17
LANE = 128
SUBLANE = 8


NORM_EPS = 1e-06
FIXED_UNIT = 1.0 / 4096.0


def shifted(value, axis, steps):
    count = lax.axis_size(axis)
    pairs = [(source, (source + steps) % count) for source in range(count)]
    return lax.ppermute(value, axis, pairs)


def ring_gather(value, axis):
    count = lax.axis_size(axis)
    ahead, behind = {0: value}, {}
    forward, backward = value, value
    for step in range(1, count // 2 + 1):
        forward = shifted(forward, axis, 1)
        behind[step] = forward
        if step < count - step:
            backward = shifted(backward, axis, -1)
            ahead[step] = backward
    return [ahead[d] if d in ahead else behind[count - d] for d in range(count)]


def slot_index(expert_ids, capacity, experts):
    flat_ids = expert_ids.reshape(-1)
    onehot = (flat_ids[:, None] == jnp.arange(experts, dtype=jnp.int32)[None, :]).astype(jnp.int32)
    before = jnp.cumsum(onehot, axis=0) - onehot
    slot_rank = jnp.sum(before * onehot, axis=1)
    return (flat_ids * capacity + slot_rank).reshape(expert_ids.shape)


def place_rows(normed, slot_ids, slot_total):
    slot_marks = slot_ids[:, :, None] == jnp.arange(slot_total, dtype=jnp.int32)[None, None, :]
    placing = jnp.sum(slot_marks.astype(jnp.float32), axis=1).T.astype(jnp.bfloat16)
    return jnp.dot(placing, normed, preferred_element_type=jnp.float32).astype(jnp.bfloat16)


def routed_branch(normed, expert_ids, route_weight, w_gate, w_up, down_all):
    n_x = lax.axis_size("ex")
    model_width = normed.shape[1]
    slot_ids = slot_index(expert_ids, MOST, EXPERTS)
    block_rows = MOST * model_width // LANE
    per_expert = place_rows(normed, slot_ids, EXPERTS * MOST).reshape(EXPERTS, block_rows, LANE)
    from_x = lax.all_to_all(per_expert, "ex", split_axis=0, concat_axis=0, tiled=True)
    held = n_x * MOST
    padded = -(-held // SUBLANE) * SUBLANE
    own_rows = jnp.pad(from_x.reshape(held, model_width), ((0, padded - held), (0, 0)))
    slot_rows = lax.all_gather(own_rows, "ey", axis=0, tiled=False)
    n_y = slot_rows.shape[0]
    flat_rows = slot_rows.reshape(-1, model_width)
    both = jnp.dot(flat_rows, w_up, preferred_element_type=jnp.float32)
    gate_act, up_act = both[:, : w_gate.shape[1]], both[:, w_gate.shape[1]:]
    hidden = (jax.nn.silu(gate_act) * up_act).astype(jnp.bfloat16)
    hidden = hidden.reshape(n_y, -1, hidden.shape[-1])[:, : n_x * MOST]
    hidden_here = lax.all_to_all(hidden, "ey", split_axis=0, concat_axis=0, tiled=True)
    me_y = lax.axis_index("ey")
    hidden_rel = jnp.take(hidden_here, (me_y + jnp.arange(n_y)) % n_y, axis=0)
    if isinstance(down_all, list):
        expert_out = None
        for d in range(n_y):
            part = jnp.dot(hidden_rel[d], down_all[d], preferred_element_type=jnp.float32)
            part = lax.reduce_precision(part, exponent_bits=8, mantissa_bits=7)
            expert_out = part if expert_out is None else expert_out + part
    else:
        parts = jnp.einsum("jrh,jhd->jrd", hidden_rel, down_all, preferred_element_type=jnp.float32)
        parts = lax.reduce_precision(parts, exponent_bits=8, mantissa_bits=7)
        expert_out = jnp.sum(parts, axis=0)
    expert_out = expert_out.reshape(n_x, block_rows, LANE)
    returned = lax.all_to_all(expert_out, "ex", split_axis=0, concat_axis=0, tiled=True)
    picked = returned.reshape(EXPERTS * MOST, model_width)[slot_ids]
    weights = route_weight.astype(jnp.float32) * FIXED_UNIT
    return jnp.sum(weights[:, :, None] * picked, axis=1)


def layer_terms(rows_in, gain_row, w_gate, w_up, down_all, expert_ids, route_weight):
    values = rows_in.astype(jnp.float32)
    inv_rms = lax.rsqrt(jnp.mean(values * values, axis=1, keepdims=True) + NORM_EPS)
    normed = (values * inv_rms * gain_row.astype(jnp.float32)).astype(jnp.bfloat16)
    branch = routed_branch(normed, expert_ids, route_weight, w_gate, w_up, down_all)
    return (values, branch)


def shards(acts, norm_gain, gate_w, up_w, down_w, route_ids, route_wts):
    section_index = lax.axis_index("pipe")
    rows_in = acts[0]
    gain_row = norm_gain[0]
    w_gate = gate_w[0, 0]
    w_up = jnp.concatenate([gate_w[0, 0], up_w[0, 0]], axis=1)
    down_all = ring_gather(down_w[0, 0], "ey")
    values, branch = layer_terms(
        rows_in, gain_row, w_gate, w_up, down_all, route_ids[0, 0], route_wts[0, 0]
    )
    first_out = (values + branch).astype(jnp.bfloat16)
    arrived = shifted(first_out, "pipe", 1)
    first_out, down_all = lax.optimization_barrier((first_out, down_all))
    down_stack = jnp.stack(down_all, axis=0)
    values, branch = layer_terms(
        arrived, gain_row, w_gate, w_up, down_stack, route_ids[0, 1], route_wts[0, 1]
    )
    second = (values + branch).astype(jnp.bfloat16)
    result_rows = jnp.where(section_index == 0, arrived, second)
    return result_rows[None]


def solution(mesh):
    n_x = EXPERTS
    n_pipe, n_expert = mesh.devices.shape
    split_mesh = Mesh(
        mesh.devices.reshape(n_pipe, n_x, n_expert // n_x), ("pipe", "ex", "ey")
    )
    rows = ("ex", "ey")
    return jax.shard_map(
        shards,
        mesh=split_mesh,
        in_specs=(
            P("pipe", rows, None),
            P("pipe", None),
            P("pipe", rows, None, None),
            P("pipe", rows, None, None),
            P("pipe", rows, None, None),
            P("pipe", None, rows, None),
            P("pipe", None, rows, None),
        ),
        out_specs=P("pipe", rows, None),
        check_vma=False,
    )
```
